128 devices in a mesh: across: 4 (over x), along: 32 (over y, z, core).
Axes of the slice: x: 4, y: 4, z: 4, core: 2. Of those that a mesh axis runs over, the one named last changes fastest.
Arguments:
- radiance: bfloat16 [224, 512, 2048], P(None, 'along', 'across'), as said below
- kernel_one: float32 [224, 25], replicated, may hold values from 0 to 0.08
- kernel_two: float32 [224, 25], replicated, may hold values from 0 to 0.08
- usable_mask: int32 [512, 2048], P('along', 'across'), may hold values from 0 to 1, as said below
Outputs:
- anomaly_score: float32 [512, 2048], P('along', 'across')
The draws below stay inside these ranges and needn't reach their ends.
Inputs may be any that keep to these rules, and one draw needn't show every extreme that they name: `usable_mask`: 1 marks a pixel that enters the statistics and is scored, 0 one that is left out. Calibrated radiance, finite.
All inputs are finite; a program needn't handle non-finite values.
Results may differ from the reference program's by a relative error of at most 0.0019.
Values may be sent and summed in bfloat16 or wider, within the bound.
No kernel may reach another device: no remote copies, remote signals or barrier semaphores. Data moves between devices by JAX's collectives and lax.ppermute only.
A program may use at most 128 MiB of HBM per device.

```python
import math
import jax
import jax.numpy as jnp
from jax import lax

BANDS = 224
KSIZE = 5
TILE_ROWS = 16
NROWS = 512
NCOLS = 2048
N_ALONG = 32


def draw_radiance(key, part):
    keys = jax.random.split(key, 4)
    base_noise = jax.random.normal(keys[0], (BANDS + 1, NROWS, NCOLS), jnp.float32)
    common_weight = 0.5
    common = jax.random.normal(keys[1], (1, NROWS, NCOLS), jnp.float32)
    band_scale = jnp.exp(jax.random.uniform(keys[2], (BANDS, 1, 1), jnp.float32, 0.0, math.log(10.0)))
    band_offset = jax.random.uniform(keys[3], (BANDS, 1, 1), jnp.float32, -1.0, 1.0)
    ramp = 1.0 + 2.0 * jnp.arange(NROWS, dtype=jnp.float32) / max(NROWS - 1, 1)
    spectra = base_noise[1:] + 0.6 * base_noise[:-1] + common_weight * common
    values = band_offset + band_scale * ramp[None, :, None] * spectra
    return values.astype(jnp.bfloat16)


def draw_usable_mask(key, part):
    ticket = jax.random.randint(key, (NROWS, NCOLS), 0, 1000)
    row_index = jnp.arange(NROWS, dtype=jnp.int32)[:, None]
    limit = 300 + 600 * row_index // max(NROWS - 1, 1)
    return (ticket < limit).astype(jnp.int32)


def setup_inputs(seed: int = 0) -> dict:
    key_list = jax.random.split(jax.random.key(seed), 5)
    radiance = draw_radiance(jax.random.fold_in(key_list[4], 71), 0)
    kernel_one = jnp.clip(jax.random.uniform(key_list[1], (BANDS, KSIZE * KSIZE), jnp.float32, 0.0, 0.08), 0.0, 0.08)
    kernel_two = jnp.clip(jax.random.uniform(key_list[2], (BANDS, KSIZE * KSIZE), jnp.float32, 0.0, 0.08), 0.0, 0.08)
    usable_mask = draw_usable_mask(jax.random.fold_in(key_list[4], 71), 0)
    return {"radiance": radiance, "kernel_one": kernel_one, "kernel_two": kernel_two, "usable_mask": usable_mask}


def smooth(padded, kernel, out_rows, out_cols):
    total = jnp.zeros((padded.shape[0], out_rows, out_cols), jnp.float32)
    for tap in range(KSIZE * KSIZE):
        row_off, col_off = divmod(tap, KSIZE)
        window = padded[:, row_off:row_off + out_rows, col_off:col_off + out_cols]
        total = total + kernel[:, tap][:, None, None] * window
    return total

def reference(radiance, kernel_one, kernel_two, usable_mask):
    band_count = radiance.shape[0]
    reach = KSIZE // 2
    widths = ((0, 0), (reach, reach), (reach, reach))

    def one_group(pieces):
        plane, first_taps, second_taps = pieces
        section_one = smooth(jnp.pad(plane.astype(jnp.float32), widths), first_taps, NROWS, NCOLS)
        section_two = smooth(jnp.pad(section_one, widths), second_taps, NROWS, NCOLS)
        return section_two.astype(jnp.bfloat16)
    groups = lax.map(one_group, (radiance.reshape(band_count // 8, 8, NROWS, NCOLS), kernel_one.reshape(band_count // 8, 8, KSIZE * KSIZE), kernel_two.reshape(band_count // 8, 8, KSIZE * KSIZE)))
    smoothed = groups.reshape(band_count, NROWS, NCOLS)
    masked = smoothed * usable_mask.astype(jnp.bfloat16)[None]
    flat = masked.reshape(band_count, NROWS * NCOLS)
    count = jnp.sum(usable_mask.astype(jnp.float32))
    band_sum = lax.optimization_barrier(jnp.sum(flat, axis=1, dtype=jnp.float32))
    gram = jnp.dot(flat.astype(jnp.float32), flat.T.astype(jnp.float32), preferred_element_type=jnp.float32)
    global_mean = band_sum / count
    covariance = (gram - count * jnp.outer(global_mean, global_mean)) / (count - 1.0)
    loading = 0.01 * jnp.trace(covariance) / band_count
    loaded = covariance + loading * jnp.eye(band_count, dtype=jnp.float32)
    lower = jnp.linalg.cholesky(loaded)
    whitener = lax.linalg.triangular_solve(lower, jnp.eye(band_count, dtype=jnp.float32), left_side=True, lower=True)

    def score_block(index):
        start = (index * TILE_ROWS).astype(jnp.int32)
        block = lax.dynamic_slice_in_dim(smoothed, start, TILE_ROWS, axis=1)
        centered = block.astype(jnp.float32).reshape(band_count, TILE_ROWS * NCOLS) - global_mean[:, None]
        whitened = jnp.dot(whitener.astype(jnp.float32), centered.astype(jnp.float32), precision=lax.Precision.HIGHEST, preferred_element_type=jnp.float32)
        return lax.optimization_barrier(jnp.sum(whitened * whitened, axis=0)).reshape(TILE_ROWS, NCOLS)
    blocks = lax.map(score_block, jnp.arange(N_ALONG, dtype=jnp.int32))
    distance = blocks.reshape(NROWS, NCOLS)
    standard = (distance - band_count) / math.sqrt(2.0 * band_count)
    return standard * usable_mask.astype(jnp.float32)
```

```python
import math

import jax
import jax.numpy as jnp
from jax import lax
from jax.experimental import pallas as pl
from jax.experimental.pallas import tpu as pltpu
from jax.sharding import PartitionSpec as P

KSIZE = 5
REACH = KSIZE // 2
HALO = 2 * REACH
LANES = 128
BAND_BLOCK = 8


def shift_pair(block, axis, dim, width):
    count = lax.axis_size(axis)
    forward = [(i, i + 1) for i in range(count - 1)]
    backward = [(target, source) for source, target in forward]
    low = lax.ppermute(
        lax.slice_in_dim(block, block.shape[dim] - width, None, axis=dim), axis, forward
    )
    high = lax.ppermute(lax.slice_in_dim(block, 0, width, axis=dim), axis, backward)
    return low, high


def smooth_kernel(k1_ref, k2_ref, mask_ref, x_ref, o_ref):
    block = pl.program_id(0)
    rows_in, cols_in = x_ref.shape[1], x_ref.shape[2]
    rows_out, cols_out = o_ref.shape[1], o_ref.shape[2]

    def correlate(x, taps, base, cols):
        total = None
        for p in range(KSIZE):
            part = None
            for q in range(KSIZE):
                xq = x if q == 0 else pltpu.roll(x, cols_in - q, 1)
                term = taps[base + p * KSIZE + q] * xq[:, :cols]
                part = term if part is None else part + term
            if p:
                part = pltpu.roll(part, rows_in - p, 0)
            total = part if total is None else total + part
        return total

    def one_band(i, carry):
        band = block * BAND_BLOCK + i
        base = band * (KSIZE * KSIZE)
        x = x_ref[i].astype(jnp.float32)
        first = correlate(x, k1_ref, base, cols_in) * mask_ref[...]
        second = correlate(first, k2_ref, base, cols_out)
        o_ref[i] = second[:rows_out].astype(o_ref.dtype)
        return carry

    lax.fori_loop(0, BAND_BLOCK, one_band, 0)


def smooth_both(padded, mask, kernel_one, kernel_two, rows_out, cols_out):
    bands, rows_in, cols_in = padded.shape
    smem = pltpu.SMEM
    return pl.pallas_call(
        smooth_kernel,
        grid=(bands // BAND_BLOCK,),
        in_specs=[
            pl.BlockSpec(memory_space=smem),
            pl.BlockSpec(memory_space=smem),
            pl.BlockSpec((rows_in, cols_in), lambda b: (0, 0)),
            pl.BlockSpec((BAND_BLOCK, rows_in, cols_in), lambda b: (b, 0, 0)),
        ],
        out_specs=pl.BlockSpec((BAND_BLOCK, rows_out, cols_out), lambda b: (b, 0, 0)),
        out_shape=jax.ShapeDtypeStruct((bands, rows_out, cols_out), jnp.bfloat16),
    )(kernel_one.reshape(-1), kernel_two.reshape(-1), mask, padded)


def tree_psum(value):
    for axis in ("along", "across"):
        size = lax.axis_size(axis)
        step = 1
        while step < size:
            pairs = [(i, i ^ step) for i in range(size)]
            value = value + lax.ppermute(value, axis, pairs)
            step *= 2
    return value


def per_device(radiance, kernel_one, kernel_two, usable_mask):
    band_count, tile_rows, tile_cols = radiance.shape
    n_across = lax.axis_size("across")
    n_along = lax.axis_size("along")
    col0 = lax.axis_index("across") * tile_cols
    row0 = lax.axis_index("along") * tile_rows

    left, right = shift_pair(radiance, "across", 2, HALO)
    wide = jnp.concatenate([left, radiance, right], axis=2)
    top, bottom = shift_pair(wide, "along", 1, HALO)
    rows_in = tile_rows + 2 * HALO
    rows_in = -(-rows_in // 8) * 8
    cols_in = -(-(tile_cols + 2 * HALO) // LANES) * LANES
    padded = jnp.concatenate([top, wide, bottom], axis=1)
    padded = jnp.pad(
        padded,
        ((0, 0), (0, rows_in - padded.shape[1]), (0, cols_in - padded.shape[2])),
    )

    mid_rows = lax.broadcasted_iota(jnp.int32, (rows_in, cols_in), 0) + (row0 - REACH)
    mid_cols = lax.broadcasted_iota(jnp.int32, (rows_in, cols_in), 1) + (col0 - REACH)
    inside = (
        (mid_rows >= 0)
        & (mid_rows < n_along * tile_rows)
        & (mid_cols >= 0)
        & (mid_cols < n_across * tile_cols)
    )
    mid_mask = inside.astype(jnp.float32)

    smoothed = smooth_both(padded, mid_mask, kernel_one, kernel_two, tile_rows, tile_cols)

    masked = smoothed * usable_mask.astype(jnp.bfloat16)[None]
    flat = masked.reshape(band_count, tile_rows * tile_cols)
    local_count = jnp.sum(usable_mask.astype(jnp.float32))
    local_sum = jnp.sum(flat, axis=1, dtype=jnp.float32)
    local_gram = lax.dot_general(
        flat, flat, (((1,), (1,)), ((), ())), preferred_element_type=jnp.float32
    )
    extra = jnp.zeros((8, band_count), jnp.float32)
    extra = extra.at[0].set(local_sum).at[1, 0].set(local_count)
    packed = tree_psum(jnp.concatenate([local_gram, extra], axis=0))
    gram = packed[:band_count]
    band_sum = packed[band_count]
    count = packed[band_count + 1, 0]

    global_mean = band_sum / count
    covariance = (gram - count * jnp.outer(global_mean, global_mean)) / (count - 1.0)
    loading = 0.01 * jnp.trace(covariance) / band_count
    loaded = covariance + loading * jnp.eye(band_count, dtype=jnp.float32)
    lower = jnp.linalg.cholesky(loaded)
    whitener = lax.linalg.triangular_solve(
        lower, jnp.eye(band_count, dtype=jnp.float32), left_side=True, lower=True
    )
    centered = (
        smoothed.astype(jnp.float32).reshape(band_count, tile_rows * tile_cols)
        - global_mean[:, None]
    )
    whitened = jnp.dot(
        whitener, centered, precision=lax.Precision.HIGHEST, preferred_element_type=jnp.float32
    )
    distance = jnp.sum(whitened * whitened, axis=0).reshape(tile_rows, tile_cols)
    standard = (distance - band_count) / math.sqrt(2.0 * band_count)
    return standard * usable_mask.astype(jnp.float32)


def solution(mesh):
    in_specs = (P(None, "along", "across"), P(), P(), P("along", "across"))
    out_specs = P("along", "across")
    return jax.shard_map(
        per_device, mesh=mesh, in_specs=in_specs, out_specs=out_specs, check_vma=False
    )
```

```python
import math

import jax
import jax.numpy as jnp
from jax import lax
from jax.experimental import pallas as pl
from jax.experimental.pallas import tpu as pltpu
from jax.sharding import PartitionSpec as P

KSIZE = 5
REACH = KSIZE // 2
HALO = 2 * REACH
LANES = 128
BAND_BLOCK = 8


def shift_pair(block, axis, dim, width):
    count = lax.axis_size(axis)
    forward = [(i, i + 1) for i in range(count - 1)]
    backward = [(target, source) for source, target in forward]
    low = lax.ppermute(
        lax.slice_in_dim(block, block.shape[dim] - width, None, axis=dim), axis, forward
    )
    high = lax.ppermute(lax.slice_in_dim(block, 0, width, axis=dim), axis, backward)
    return low, high


def smooth_kernel(k1_ref, k2_ref, mask_ref, x_ref, tb_ref, side_ref, o_ref, grid_ref):
    block = pl.program_id(0)
    rows_in, cols_in = grid_ref.shape
    rows_out, cols_out = o_ref.shape[1], o_ref.shape[2]

    def correlate(x, taps, base, cols):
        total = None
        for p in range(KSIZE):
            part = None
            for q in range(KSIZE):
                shift = (REACH - q) % cols_in
                xq = pltpu.roll(x, shift, 1) if shift else x
                term = taps[base + p * KSIZE + q] * xq[:, :cols]
                part = term if part is None else part + term
            shift = (REACH - p) % rows_in
            if shift:
                part = pltpu.roll(part, shift, 0)
            total = part if total is None else total + part
        return total

    def one_band(i, carry):
        band = block * BAND_BLOCK + i
        base = band * (KSIZE * KSIZE)
        grid_ref[:rows_out, :cols_out] = x_ref[i].astype(jnp.float32)
        grid_ref[rows_out:, :cols_out] = tb_ref[i].astype(jnp.float32)
        grid_ref[:, cols_out:] = side_ref[i].astype(jnp.float32)
        x = grid_ref[...]
        first = correlate(x, k1_ref, base, cols_in) * mask_ref[...]
        second = correlate(first, k2_ref, base, cols_out)
        o_ref[i] = second[:rows_out].astype(o_ref.dtype)
        return carry

    lax.fori_loop(0, BAND_BLOCK, one_band, 0)


def smooth_both(center, tb, side, mask, kernel_one, kernel_two):
    bands, rows_out, cols_out = center.shape
    rows_in, cols_in = mask.shape
    smem = pltpu.SMEM
    return pl.pallas_call(
        smooth_kernel,
        grid=(bands // BAND_BLOCK,),
        in_specs=[
            pl.BlockSpec(memory_space=smem),
            pl.BlockSpec(memory_space=smem),
            pl.BlockSpec((rows_in, cols_in), lambda b: (0, 0)),
            pl.BlockSpec((BAND_BLOCK, rows_out, cols_out), lambda b: (b, 0, 0)),
            pl.BlockSpec((BAND_BLOCK, tb.shape[1], cols_out), lambda b: (b, 0, 0)),
            pl.BlockSpec((BAND_BLOCK, rows_in, side.shape[2]), lambda b: (b, 0, 0)),
        ],
        out_specs=pl.BlockSpec((BAND_BLOCK, rows_out, cols_out), lambda b: (b, 0, 0)),
        out_shape=jax.ShapeDtypeStruct((bands, rows_out, cols_out), jnp.bfloat16),
        scratch_shapes=[pltpu.VMEM((rows_in, cols_in), jnp.float32)],
    )(kernel_one.reshape(-1), kernel_two.reshape(-1), mask, center, tb, side)


def tree_psum(value):
    for axis in ("along", "across"):
        size = lax.axis_size(axis)
        step = 1
        while step < size:
            pairs = [(i, i ^ step) for i in range(size)]
            value = value + lax.ppermute(value, axis, pairs)
            step *= 2
    return value


def per_device(radiance, kernel_one, kernel_two, usable_mask):
    band_count, tile_rows, tile_cols = radiance.shape
    n_across = lax.axis_size("across")
    n_along = lax.axis_size("along")
    col0 = lax.axis_index("across") * tile_cols
    row0 = lax.axis_index("along") * tile_rows

    top, bottom = shift_pair(radiance, "along", 1, HALO)
    tall = jnp.concatenate([radiance, bottom, top], axis=1)
    left, right = shift_pair(tall, "across", 2, HALO)
    rows_in = tall.shape[1]
    gap = LANES - 2 * HALO
    side = jnp.concatenate(
        [right, jnp.zeros((band_count, rows_in, gap), right.dtype), left], axis=2
    )
    tb = jnp.concatenate([bottom, top], axis=1)
    cols_in = tile_cols + LANES

    pos_rows = lax.broadcasted_iota(jnp.int32, (rows_in, cols_in), 0)
    pos_cols = lax.broadcasted_iota(jnp.int32, (rows_in, cols_in), 1)
    mid_rows = jnp.where(pos_rows < tile_rows + HALO, pos_rows, pos_rows - rows_in) + row0
    mid_cols = jnp.where(pos_cols < tile_cols + LANES // 2, pos_cols, pos_cols - cols_in) + col0
    inside = (
        (mid_rows >= 0)
        & (mid_rows < n_along * tile_rows)
        & (mid_cols >= 0)
        & (mid_cols < n_across * tile_cols)
    )
    mid_mask = inside.astype(jnp.float32)

    smoothed = smooth_both(radiance, tb, side, mid_mask, kernel_one, kernel_two)

    masked = smoothed * usable_mask.astype(jnp.bfloat16)[None]
    flat = masked.reshape(band_count, tile_rows * tile_cols)
    local_count = jnp.sum(usable_mask.astype(jnp.float32))
    local_sum = jnp.sum(flat, axis=1, dtype=jnp.float32)
    local_gram = lax.dot_general(
        flat, flat, (((1,), (1,)), ((), ())), preferred_element_type=jnp.float32
    )
    half = band_count // 2
    upper_a = local_gram[:half, :half]
    lower_c = local_gram[half:, half:]
    below = lax.broadcasted_iota(jnp.int32, (half, half), 0) >= lax.broadcasted_iota(
        jnp.int32, (half, half), 1
    )
    folded = jnp.where(below, upper_a, lower_c)
    extra = jnp.zeros((8, band_count), jnp.float32)
    extra = extra.at[0].set(local_sum).at[1, 0].set(local_count)
    extra = extra.at[2, :half].set(jnp.diagonal(lower_c))
    body = jnp.concatenate([local_gram[half:, :half], folded], axis=1)
    packed = tree_psum(jnp.concatenate([body, extra], axis=0))
    cross = packed[:half, :half]
    folded = packed[:half, half:]
    strict = jnp.where(below, folded, 0.0)
    strict_low = strict - jnp.diag(jnp.diagonal(folded))
    block_a = strict + strict_low.T
    strict_up = jnp.where(below, 0.0, folded)
    block_c = strict_up + strict_up.T + jnp.diag(packed[half + 2, :half])
    gram = jnp.concatenate(
        [
            jnp.concatenate([block_a, cross.T], axis=1),
            jnp.concatenate([cross, block_c], axis=1),
        ],
        axis=0,
    )
    band_sum = packed[half]
    count = packed[half + 1, 0]

    global_mean = band_sum / count
    covariance = (gram - count * jnp.outer(global_mean, global_mean)) / (count - 1.0)
    loading = 0.01 * jnp.trace(covariance) / band_count
    loaded = covariance + loading * jnp.eye(band_count, dtype=jnp.float32)
    lower = jnp.linalg.cholesky(loaded)
    whitener = lax.linalg.triangular_solve(
        lower, jnp.eye(band_count, dtype=jnp.float32), left_side=True, lower=True
    )
    centered = (
        smoothed.astype(jnp.float32).reshape(band_count, tile_rows * tile_cols)
        - global_mean[:, None]
    )
    whitened = jnp.dot(
        whitener, centered, precision=lax.Precision.HIGHEST, preferred_element_type=jnp.float32
    )
    distance = jnp.sum(whitened * whitened, axis=0).reshape(tile_rows, tile_cols)
    standard = (distance - band_count) / math.sqrt(2.0 * band_count)
    return standard * usable_mask.astype(jnp.float32)


def solution(mesh):
    in_specs = (P(None, "along", "across"), P(), P(), P("along", "across"))
    out_specs = P("along", "across")
    return jax.shard_map(
        per_device, mesh=mesh, in_specs=in_specs, out_specs=out_specs, check_vma=False
    )
```

```python
import math

import jax
import jax.numpy as jnp
from jax import lax
from jax.experimental import pallas as pl
from jax.experimental.pallas import tpu as pltpu
from jax.sharding import PartitionSpec as P

KSIZE = 5
REACH = KSIZE // 2
HALO = 2 * REACH
LANES = 128
BAND_BLOCK = 8


def shift_pair(block, axis, dim, width):
    count = lax.axis_size(axis)
    forward = [(i, i + 1) for i in range(count - 1)]
    backward = [(target, source) for source, target in forward]
    low = lax.ppermute(
        lax.slice_in_dim(block, block.shape[dim] - width, None, axis=dim), axis, forward
    )
    high = lax.ppermute(lax.slice_in_dim(block, 0, width, axis=dim), axis, backward)
    return low, high


def smooth_kernel(k1_ref, k2_ref, mask_ref, x_ref, tb_ref, side_ref, o_ref, grid_ref):
    block = pl.program_id(0)
    rows_in, cols_in = grid_ref.shape
    rows_out, cols_out = o_ref.shape[1], o_ref.shape[2]

    def correlate(x, taps, base, cols):
        total = None
        for p in range(KSIZE):
            part = None
            for q in range(KSIZE):
                shift = (REACH - q) % cols_in
                xq = pltpu.roll(x, shift, 1) if shift else x
                term = taps[base + p * KSIZE + q] * xq[:, :cols]
                part = term if part is None else part + term
            shift = (REACH - p) % rows_in
            if shift:
                part = pltpu.roll(part, shift, 0)
            total = part if total is None else total + part
        return total

    def one_band(i, carry):
        band = block * BAND_BLOCK + i
        base = band * (KSIZE * KSIZE)
        grid_ref[:rows_out, :cols_out] = x_ref[i].astype(jnp.float32)
        grid_ref[rows_out:, :cols_out] = tb_ref[i].astype(jnp.float32)
        grid_ref[:, cols_out:] = side_ref[i].astype(jnp.float32)
        x = grid_ref[...]
        first = correlate(x, k1_ref, base, cols_in) * mask_ref[...]
        second = correlate(first, k2_ref, base, cols_out)
        o_ref[i] = second[:rows_out].astype(o_ref.dtype)
        return carry

    lax.fori_loop(0, BAND_BLOCK, one_band, 0)


def smooth_both(center, tb, side, mask, kernel_one, kernel_two):
    bands, rows_out, cols_out = center.shape
    rows_in, cols_in = mask.shape
    smem = pltpu.SMEM
    return pl.pallas_call(
        smooth_kernel,
        grid=(bands // BAND_BLOCK,),
        in_specs=[
            pl.BlockSpec(memory_space=smem),
            pl.BlockSpec(memory_space=smem),
            pl.BlockSpec((rows_in, cols_in), lambda b: (0, 0)),
            pl.BlockSpec((BAND_BLOCK, rows_out, cols_out), lambda b: (b, 0, 0)),
            pl.BlockSpec((BAND_BLOCK, tb.shape[1], cols_out), lambda b: (b, 0, 0)),
            pl.BlockSpec((BAND_BLOCK, rows_in, side.shape[2]), lambda b: (b, 0, 0)),
        ],
        out_specs=pl.BlockSpec((BAND_BLOCK, rows_out, cols_out), lambda b: (b, 0, 0)),
        out_shape=jax.ShapeDtypeStruct((bands, rows_out, cols_out), jnp.bfloat16),
        scratch_shapes=[pltpu.VMEM((rows_in, cols_in), jnp.float32)],
    )(kernel_one.reshape(-1), kernel_two.reshape(-1), mask, center, tb, side)


def tree_psum(value):
    for axis in ("along", "across"):
        size = lax.axis_size(axis)
        step = 1
        while step < size:
            pairs = [(i, i ^ step) for i in range(size)]
            value = value + lax.ppermute(value, axis, pairs)
            step *= 2
    return value


def per_device(radiance, kernel_one, kernel_two, usable_mask):
    band_count, tile_rows, tile_cols = radiance.shape
    n_across = lax.axis_size("across")
    n_along = lax.axis_size("along")
    col0 = lax.axis_index("across") * tile_cols
    row0 = lax.axis_index("along") * tile_rows

    top, bottom = shift_pair(radiance, "along", 1, HALO)
    left, right = shift_pair(radiance, "across", 2, HALO)
    top_left, bottom_left = shift_pair(left, "along", 1, HALO)
    top_right, bottom_right = shift_pair(right, "along", 1, HALO)
    rows_in = tile_rows + 2 * HALO
    gap = LANES - 2 * HALO
    side = jnp.concatenate(
        [
            jnp.concatenate([right, bottom_right, top_right], axis=1),
            jnp.zeros((band_count, rows_in, gap), radiance.dtype),
            jnp.concatenate([left, bottom_left, top_left], axis=1),
        ],
        axis=2,
    )
    tb = jnp.concatenate([bottom, top], axis=1)
    cols_in = tile_cols + LANES

    pos_rows = lax.broadcasted_iota(jnp.int32, (rows_in, cols_in), 0)
    pos_cols = lax.broadcasted_iota(jnp.int32, (rows_in, cols_in), 1)
    mid_rows = jnp.where(pos_rows < tile_rows + HALO, pos_rows, pos_rows - rows_in) + row0
    mid_cols = jnp.where(pos_cols < tile_cols + LANES // 2, pos_cols, pos_cols - cols_in) + col0
    inside = (
        (mid_rows >= 0)
        & (mid_rows < n_along * tile_rows)
        & (mid_cols >= 0)
        & (mid_cols < n_across * tile_cols)
    )
    mid_mask = inside.astype(jnp.float32)

    smoothed = smooth_both(radiance, tb, side, mid_mask, kernel_one, kernel_two)

    masked = smoothed * usable_mask.astype(jnp.bfloat16)[None]
    flat = masked.reshape(band_count, tile_rows * tile_cols)
    local_count = jnp.sum(usable_mask.astype(jnp.float32))
    local_sum = jnp.sum(flat, axis=1, dtype=jnp.float32)
    local_gram = lax.dot_general(
        flat, flat, (((1,), (1,)), ((), ())), preferred_element_type=jnp.float32
    )
    half = band_count // 2
    upper_a = local_gram[:half, :half]
    lower_c = local_gram[half:, half:]
    below = lax.broadcasted_iota(jnp.int32, (half, half), 0) >= lax.broadcasted_iota(
        jnp.int32, (half, half), 1
    )
    folded = jnp.where(below, upper_a, lower_c)
    extra = jnp.zeros((8, band_count), jnp.float32)
    extra = extra.at[0].set(local_sum).at[1, 0].set(local_count)
    extra = extra.at[2, :half].set(jnp.diagonal(lower_c))
    body = jnp.concatenate([local_gram[half:, :half], folded], axis=1)
    packed = tree_psum(jnp.concatenate([body, extra], axis=0))
    cross = packed[:half, :half]
    folded = packed[:half, half:]
    strict = jnp.where(below, folded, 0.0)
    strict_low = strict - jnp.diag(jnp.diagonal(folded))
    block_a = strict + strict_low.T
    strict_up = jnp.where(below, 0.0, folded)
    block_c = strict_up + strict_up.T + jnp.diag(packed[half + 2, :half])
    gram = jnp.concatenate(
        [
            jnp.concatenate([block_a, cross.T], axis=1),
            jnp.concatenate([cross, block_c], axis=1),
        ],
        axis=0,
    )
    band_sum = packed[half]
    count = packed[half + 1, 0]

    global_mean = band_sum / count
    covariance = (gram - count * jnp.outer(global_mean, global_mean)) / (count - 1.0)
    loading = 0.01 * jnp.trace(covariance) / band_count
    loaded = covariance + loading * jnp.eye(band_count, dtype=jnp.float32)
    lower = jnp.linalg.cholesky(loaded)
    whitener = lax.linalg.triangular_solve(
        lower, jnp.eye(band_count, dtype=jnp.float32), left_side=True, lower=True
    )
    centered = (
        smoothed.astype(jnp.float32).reshape(band_count, tile_rows * tile_cols)
        - global_mean[:, None]
    )
    whitened = jnp.dot(
        whitener, centered, precision=lax.Precision.HIGH, preferred_element_type=jnp.float32
    )
    distance = jnp.sum(whitened * whitened, axis=0).reshape(tile_rows, tile_cols)
    standard = (distance - band_count) / math.sqrt(2.0 * band_count)
    return standard * usable_mask.astype(jnp.float32)


def solution(mesh):
    in_specs = (P(None, "along", "across"), P(), P(), P("along", "across"))
    out_specs = P("along", "across")
    return jax.shard_map(
        per_device, mesh=mesh, in_specs=in_specs, out_specs=out_specs, check_vma=False
    )
```

```python
import functools
import math

import jax
import jax.numpy as jnp
from jax import lax
from jax.experimental import pallas as pl
from jax.experimental.pallas import tpu as pltpu
from jax.sharding import PartitionSpec as P

KSIZE = 5
REACH = KSIZE // 2
HALO = 2 * REACH
LANES = 128
BAND_BLOCK = 8
CHUNKS = 2
UNROLL = 1


def shift_pair(block, axis, dim, width):
    count = lax.axis_size(axis)
    forward = [(i, i + 1) for i in range(count - 1)]
    backward = [(target, source) for source, target in forward]
    low = lax.ppermute(
        lax.slice_in_dim(block, block.shape[dim] - width, None, axis=dim), axis, forward
    )
    high = lax.ppermute(lax.slice_in_dim(block, 0, width, axis=dim), axis, backward)
    return low, high


def smooth_kernel(first_block, k1_ref, k2_ref, mask_ref, x_ref, tb_ref, side_ref, *refs):
    o_ref, grid_ref = refs[-2], refs[-1]
    block = pl.program_id(0) + first_block
    rows_in, cols_in = grid_ref.shape
    rows_out, cols_out = o_ref.shape[1], o_ref.shape[2]

    def correlate(x, taps, base, cols):
        total = None
        for p in range(KSIZE):
            part = None
            for q in range(KSIZE):
                shift = (REACH - q) % cols_in
                xq = pltpu.roll(x, shift, 1) if shift else x
                term = taps[base + p * KSIZE + q] * xq[:, :cols]
                part = term if part is None else part + term
            shift = (REACH - p) % rows_in
            if shift:
                part = pltpu.roll(part, shift, 0)
            total = part if total is None else total + part
        return total

    def one_band(i, carry):
        base = (block * BAND_BLOCK + i) * (KSIZE * KSIZE)
        grid_ref[:rows_out, :cols_out] = x_ref[i].astype(jnp.float32)
        grid_ref[rows_out:, :cols_out] = tb_ref[i].astype(jnp.float32)
        grid_ref[:, cols_out:] = side_ref[i].astype(jnp.float32)
        x = grid_ref[...]
        first = correlate(x, k1_ref, base, cols_in) * mask_ref[...]
        second = correlate(first, k2_ref, base, cols_out)
        o_ref[i] = second[:rows_out].astype(o_ref.dtype)
        return carry

    lax.fori_loop(0, BAND_BLOCK, one_band, 0, unroll=UNROLL)


def smooth_both(center, first_band, tb, side, mask, kernel_one, kernel_two, previous=None):
    bands, rows_out, cols_out = center.shape
    rows_in, cols_in = mask.shape
    first_block = first_band // BAND_BLOCK
    smem = pltpu.SMEM
    in_specs = [
        pl.BlockSpec(memory_space=smem),
        pl.BlockSpec(memory_space=smem),
        pl.BlockSpec((rows_in, cols_in), lambda b: (0, 0)),
        pl.BlockSpec((BAND_BLOCK, rows_out, cols_out), lambda b: (b + first_block, 0, 0)),
        pl.BlockSpec((BAND_BLOCK, tb.shape[1], cols_out), lambda b: (b, 0, 0)),
        pl.BlockSpec((BAND_BLOCK, rows_in, side.shape[2]), lambda b: (b, 0, 0)),
    ]
    operands = [kernel_one.reshape(-1), kernel_two.reshape(-1), mask, center, tb, side]
    aliases = {}
    if previous is not None:
        in_specs.append(pl.BlockSpec(memory_space=pl.ANY))
        operands.append(previous)
        aliases = {len(operands) - 1: 0}
    return pl.pallas_call(
        functools.partial(smooth_kernel, first_block),
        grid=(tb.shape[0] // BAND_BLOCK,),
        in_specs=in_specs,
        out_specs=pl.BlockSpec(
            (BAND_BLOCK, rows_out, cols_out), lambda b: (b + first_block, 0, 0)
        ),
        out_shape=jax.ShapeDtypeStruct((bands, rows_out, cols_out), jnp.bfloat16),
        scratch_shapes=[pltpu.VMEM((rows_in, cols_in), jnp.float32)],
        input_output_aliases=aliases,
    )(*operands)


def halo_pieces(chunk):
    band_count, tile_rows, tile_cols = chunk.shape
    top, bottom = shift_pair(chunk, "along", 1, HALO)
    left, right = shift_pair(chunk, "across", 2, HALO)
    top_left, bottom_left = shift_pair(left, "along", 1, HALO)
    top_right, bottom_right = shift_pair(right, "along", 1, HALO)
    rows_in = tile_rows + 2 * HALO
    gap = LANES - 2 * HALO
    side = jnp.concatenate(
        [
            jnp.concatenate([right, bottom_right, top_right], axis=1),
            jnp.zeros((band_count, rows_in, gap), chunk.dtype),
            jnp.concatenate([left, bottom_left, top_left], axis=1),
        ],
        axis=2,
    )
    tb = jnp.concatenate([bottom, top], axis=1)
    return tb, side


def tree_psum(value):
    for axis in ("along", "across"):
        size = lax.axis_size(axis)
        step = 1
        while step < size:
            pairs = [(i, i ^ step) for i in range(size)]
            value = value + lax.ppermute(value, axis, pairs)
            step *= 2
    return value


def per_device(radiance, kernel_one, kernel_two, usable_mask):
    band_count, tile_rows, tile_cols = radiance.shape
    n_across = lax.axis_size("across")
    n_along = lax.axis_size("along")
    col0 = lax.axis_index("across") * tile_cols
    row0 = lax.axis_index("along") * tile_rows

    rows_in = tile_rows + 2 * HALO
    cols_in = tile_cols + LANES

    pos_rows = lax.broadcasted_iota(jnp.int32, (rows_in, cols_in), 0)
    pos_cols = lax.broadcasted_iota(jnp.int32, (rows_in, cols_in), 1)
    mid_rows = jnp.where(pos_rows < tile_rows + HALO, pos_rows, pos_rows - rows_in) + row0
    mid_cols = jnp.where(pos_cols < tile_cols + LANES // 2, pos_cols, pos_cols - cols_in) + col0
    inside = (
        (mid_rows >= 0)
        & (mid_rows < n_along * tile_rows)
        & (mid_cols >= 0)
        & (mid_cols < n_across * tile_cols)
    )
    mid_mask = inside.astype(jnp.float32)

    chunk = band_count // CHUNKS
    smoothed = None
    for c in range(CHUNKS):
        tb, side = halo_pieces(radiance[c * chunk : (c + 1) * chunk])
        smoothed = smooth_both(
            radiance, c * chunk, tb, side, mid_mask, kernel_one, kernel_two, smoothed
        )

    masked = smoothed * usable_mask.astype(jnp.bfloat16)[None]
    flat = masked.reshape(band_count, tile_rows * tile_cols)
    local_count = jnp.sum(usable_mask.astype(jnp.float32))
    local_sum = jnp.sum(flat, axis=1, dtype=jnp.float32)
    local_gram = lax.dot_general(
        flat, flat, (((1,), (1,)), ((), ())), preferred_element_type=jnp.float32
    )
    half = band_count // 2
    upper_a = local_gram[:half, :half]
    lower_c = local_gram[half:, half:]
    below = lax.broadcasted_iota(jnp.int32, (half, half), 0) >= lax.broadcasted_iota(
        jnp.int32, (half, half), 1
    )
    folded = jnp.where(below, upper_a, lower_c)
    extra = jnp.zeros((8, band_count), jnp.float32)
    extra = extra.at[0].set(local_sum).at[1, 0].set(local_count)
    extra = extra.at[2, :half].set(jnp.diagonal(lower_c))
    body = jnp.concatenate([local_gram[half:, :half], folded], axis=1)
    packed = tree_psum(jnp.concatenate([body, extra], axis=0))
    cross = packed[:half, :half]
    folded = packed[:half, half:]
    strict = jnp.where(below, folded, 0.0)
    strict_low = strict - jnp.diag(jnp.diagonal(folded))
    block_a = strict + strict_low.T
    strict_up = jnp.where(below, 0.0, folded)
    block_c = strict_up + strict_up.T + jnp.diag(packed[half + 2, :half])
    gram = jnp.concatenate(
        [
            jnp.concatenate([block_a, cross.T], axis=1),
            jnp.concatenate([cross, block_c], axis=1),
        ],
        axis=0,
    )
    band_sum = packed[half]
    count = packed[half + 1, 0]

    global_mean = band_sum / count
    covariance = (gram - count * jnp.outer(global_mean, global_mean)) / (count - 1.0)
    loading = 0.01 * jnp.trace(covariance) / band_count
    loaded = covariance + loading * jnp.eye(band_count, dtype=jnp.float32)
    lower = jnp.linalg.cholesky(loaded)
    whitener = lax.linalg.triangular_solve(
        lower, jnp.eye(band_count, dtype=jnp.float32), left_side=True, lower=True
    )
    centered = (
        smoothed.astype(jnp.float32).reshape(band_count, tile_rows * tile_cols)
        - global_mean[:, None]
    )
    whitened = jnp.dot(
        whitener, centered, precision=lax.Precision.HIGH, preferred_element_type=jnp.float32
    )
    distance = jnp.sum(whitened * whitened, axis=0).reshape(tile_rows, tile_cols)
    standard = (distance - band_count) / math.sqrt(2.0 * band_count)
    return standard * usable_mask.astype(jnp.float32)


def solution(mesh):
    in_specs = (P(None, "along", "across"), P(), P(), P("along", "across"))
    out_specs = P("along", "across")
    return jax.shard_map(
        per_device, mesh=mesh, in_specs=in_specs, out_specs=out_specs, check_vma=False
    )
```

```python
import math

import jax
import jax.numpy as jnp
from jax import lax
from jax.experimental import pallas as pl
from jax.experimental.pallas import tpu as pltpu
from jax.sharding import PartitionSpec as P

KSIZE = 5
REACH = KSIZE // 2
HALO = 2 * REACH
LANES = 128
BAND_BLOCK = 8
UNROLL = 2


def shift_pair(block, axis, dim, width):
    count = lax.axis_size(axis)
    forward = [(i, i + 1) for i in range(count - 1)]
    backward = [(target, source) for source, target in forward]
    low = lax.ppermute(
        lax.slice_in_dim(block, block.shape[dim] - width, None, axis=dim), axis, forward
    )
    high = lax.ppermute(lax.slice_in_dim(block, 0, width, axis=dim), axis, backward)
    return low, high


def smooth_kernel(
    k1_ref, k2_ref, mask_ref, use_ref, x_ref, tb_ref, side_ref, o_ref, m_ref, s_ref, grid_ref
):
    block = pl.program_id(0)
    rows_in, cols_in = grid_ref.shape
    rows_out, cols_out = o_ref.shape[1], o_ref.shape[2]

    def correlate(x, taps, base, cols):
        total = None
        for p in range(KSIZE):
            part = None
            for q in range(KSIZE):
                shift = (REACH - q) % cols_in
                xq = pltpu.roll(x, shift, 1) if shift else x
                term = taps[base + p * KSIZE + q] * xq[:, :cols]
                part = term if part is None else part + term
            shift = (REACH - p) % rows_in
            if shift:
                part = pltpu.roll(part, shift, 0)
            total = part if total is None else total + part
        return total

    def one_band(i, carry):
        band = block * BAND_BLOCK + i
        base = band * (KSIZE * KSIZE)
        grid_ref[:rows_out, :cols_out] = x_ref[i].astype(jnp.float32)
        grid_ref[rows_out:, :cols_out] = tb_ref[i].astype(jnp.float32)
        grid_ref[:, cols_out:] = side_ref[i].astype(jnp.float32)
        x = grid_ref[...]
        first = correlate(x, k1_ref, base, cols_in) * mask_ref[...]
        second = correlate(first, k2_ref, base, cols_out)
        smooth = second[:rows_out].astype(o_ref.dtype)
        o_ref[i] = smooth
        masked = smooth * use_ref[...]
        m_ref[i] = masked
        wide = masked.astype(jnp.float32)
        partial = wide[0:8]
        for r in range(8, rows_out, 8):
            partial = partial + wide[r : r + 8]
        lanes = partial[:, 0:LANES]
        for c in range(LANES, cols_out, LANES):
            lanes = lanes + partial[:, c : c + LANES]
        s_ref[i] = lanes
        return carry

    lax.fori_loop(0, BAND_BLOCK, one_band, 0, unroll=UNROLL)


def smooth_both(center, tb, side, mask, use, kernel_one, kernel_two):
    bands, rows_out, cols_out = center.shape
    rows_in, cols_in = mask.shape
    smem = pltpu.SMEM
    return pl.pallas_call(
        smooth_kernel,
        grid=(bands // BAND_BLOCK,),
        in_specs=[
            pl.BlockSpec(memory_space=smem),
            pl.BlockSpec(memory_space=smem),
            pl.BlockSpec((rows_in, cols_in), lambda b: (0, 0)),
            pl.BlockSpec((rows_out, cols_out), lambda b: (0, 0)),
            pl.BlockSpec((BAND_BLOCK, rows_out, cols_out), lambda b: (b, 0, 0)),
            pl.BlockSpec((BAND_BLOCK, tb.shape[1], cols_out), lambda b: (b, 0, 0)),
            pl.BlockSpec((BAND_BLOCK, rows_in, side.shape[2]), lambda b: (b, 0, 0)),
        ],
        out_specs=[
            pl.BlockSpec((BAND_BLOCK, rows_out, cols_out), lambda b: (b, 0, 0)),
            pl.BlockSpec((BAND_BLOCK, rows_out, cols_out), lambda b: (b, 0, 0)),
            pl.BlockSpec((BAND_BLOCK, 8, LANES), lambda b: (b, 0, 0)),
        ],
        out_shape=[
            jax.ShapeDtypeStruct((bands, rows_out, cols_out), jnp.bfloat16),
            jax.ShapeDtypeStruct((bands, rows_out, cols_out), jnp.bfloat16),
            jax.ShapeDtypeStruct((bands, 8, LANES), jnp.float32),
        ],
        scratch_shapes=[pltpu.VMEM((rows_in, cols_in), jnp.float32)],
    )(kernel_one.reshape(-1), kernel_two.reshape(-1), mask, use, center, tb, side)


def tree_psum(value):
    for axis in ("along", "across"):
        size = lax.axis_size(axis)
        step = 1
        while step < size:
            pairs = [(i, i ^ step) for i in range(size)]
            value = value + lax.ppermute(value, axis, pairs)
            step *= 2
    return value


def per_device(radiance, kernel_one, kernel_two, usable_mask):
    band_count, tile_rows, tile_cols = radiance.shape
    n_across = lax.axis_size("across")
    n_along = lax.axis_size("along")
    col0 = lax.axis_index("across") * tile_cols
    row0 = lax.axis_index("along") * tile_rows

    top, bottom = shift_pair(radiance, "along", 1, HALO)
    tall = jnp.concatenate([radiance, bottom, top], axis=1)
    left, right = shift_pair(tall, "across", 2, HALO)
    rows_in = tall.shape[1]
    gap = LANES - 2 * HALO
    side = jnp.concatenate(
        [right, jnp.zeros((band_count, rows_in, gap), right.dtype), left], axis=2
    )
    tb = jnp.concatenate([bottom, top], axis=1)
    cols_in = tile_cols + LANES

    pos_rows = lax.broadcasted_iota(jnp.int32, (rows_in, cols_in), 0)
    pos_cols = lax.broadcasted_iota(jnp.int32, (rows_in, cols_in), 1)
    mid_rows = jnp.where(pos_rows < tile_rows + HALO, pos_rows, pos_rows - rows_in) + row0
    mid_cols = jnp.where(pos_cols < tile_cols + LANES // 2, pos_cols, pos_cols - cols_in) + col0
    inside = (
        (mid_rows >= 0)
        & (mid_rows < n_along * tile_rows)
        & (mid_cols >= 0)
        & (mid_cols < n_across * tile_cols)
    )
    mid_mask = inside.astype(jnp.float32)

    use = usable_mask.astype(jnp.bfloat16)
    smoothed, masked, partial = smooth_both(
        radiance, tb, side, mid_mask, use, kernel_one, kernel_two
    )
    flat = masked.reshape(band_count, tile_rows * tile_cols)
    local_count = jnp.sum(usable_mask.astype(jnp.float32))
    local_sum = jnp.sum(partial, axis=(1, 2))
    local_gram = lax.dot_general(
        flat, flat, (((1,), (1,)), ((), ())), preferred_element_type=jnp.float32
    )
    half = band_count // 2
    upper_a = local_gram[:half, :half]
    lower_c = local_gram[half:, half:]
    below = lax.broadcasted_iota(jnp.int32, (half, half), 0) >= lax.broadcasted_iota(
        jnp.int32, (half, half), 1
    )
    folded = jnp.where(below, upper_a, lower_c)
    extra = jnp.zeros((8, band_count), jnp.float32)
    extra = extra.at[0].set(local_sum).at[1, 0].set(local_count)
    extra = extra.at[2, :half].set(jnp.diagonal(lower_c))
    body = jnp.concatenate([local_gram[half:, :half], folded], axis=1)
    packed = tree_psum(jnp.concatenate([body, extra], axis=0))
    cross = packed[:half, :half]
    folded = packed[:half, half:]
    strict = jnp.where(below, folded, 0.0)
    strict_low = strict - jnp.diag(jnp.diagonal(folded))
    block_a = strict + strict_low.T
    strict_up = jnp.where(below, 0.0, folded)
    block_c = strict_up + strict_up.T + jnp.diag(packed[half + 2, :half])
    gram = jnp.concatenate(
        [
            jnp.concatenate([block_a, cross.T], axis=1),
            jnp.concatenate([cross, block_c], axis=1),
        ],
        axis=0,
    )
    band_sum = packed[half]
    count = packed[half + 1, 0]

    global_mean = band_sum / count
    covariance = (gram - count * jnp.outer(global_mean, global_mean)) / (count - 1.0)
    loading = 0.01 * jnp.trace(covariance) / band_count
    loaded = covariance + loading * jnp.eye(band_count, dtype=jnp.float32)
    lower = jnp.linalg.cholesky(loaded)
    whitener = lax.linalg.triangular_solve(
        lower, jnp.eye(band_count, dtype=jnp.float32), left_side=True, lower=True
    )
    centered = (
        smoothed.astype(jnp.float32).reshape(band_count, tile_rows * tile_cols)
        - global_mean[:, None]
    )
    whitened = jnp.dot(
        whitener, centered, precision=lax.Precision.HIGH, preferred_element_type=jnp.float32
    )
    distance = jnp.sum(whitened * whitened, axis=0).reshape(tile_rows, tile_cols)
    standard = (distance - band_count) / math.sqrt(2.0 * band_count)
    return standard * usable_mask.astype(jnp.float32)


def solution(mesh):
    in_specs = (P(None, "along", "across"), P(), P(), P("along", "across"))
    out_specs = P("along", "across")
    return jax.shard_map(
        per_device, mesh=mesh, in_specs=in_specs, out_specs=out_specs, check_vma=False
    )
```

```python
import math

import jax
import jax.numpy as jnp
from jax import lax
from jax.experimental import pallas as pl
from jax.experimental.pallas import tpu as pltpu
from jax.sharding import PartitionSpec as P

KSIZE = 5
REACH = KSIZE // 2
HALO = 2 * REACH
LANES = 128
BAND_BLOCK = 8
UNROLL = 2


def shift_pair(block, axis, dim, width):
    count = lax.axis_size(axis)
    forward = [(i, i + 1) for i in range(count - 1)]
    backward = [(target, source) for source, target in forward]
    low = lax.ppermute(
        lax.slice_in_dim(block, block.shape[dim] - width, None, axis=dim), axis, forward
    )
    high = lax.ppermute(lax.slice_in_dim(block, 0, width, axis=dim), axis, backward)
    return low, high


def smooth_kernel(
    k1_ref, k2_ref, mask_ref, use_ref, x_ref, tb_ref, side_ref, o_ref, m_ref, s_ref, grid_ref
):
    block = pl.program_id(0)
    rows_in, cols_in = grid_ref.shape
    rows_out, cols_out = o_ref.shape[1], o_ref.shape[2]

    def correlate(x, taps, base, cols):
        total = None
        for p in range(KSIZE):
            part = None
            for q in range(KSIZE):
                shift = (REACH - q) % cols_in
                xq = pltpu.roll(x, shift, 1) if shift else x
                term = taps[base + p * KSIZE + q] * xq[:, :cols]
                part = term if part is None else part + term
            shift = (REACH - p) % rows_in
            if shift:
                part = pltpu.roll(part, shift, 0)
            total = part if total is None else total + part
        return total

    def one_band(i, carry):
        band = block * BAND_BLOCK + i
        base = band * (KSIZE * KSIZE)
        grid_ref[:rows_out, :cols_out] = x_ref[i].astype(jnp.float32)
        grid_ref[rows_out:, :cols_out] = tb_ref[i].astype(jnp.float32)
        grid_ref[:, cols_out:] = side_ref[i].astype(jnp.float32)
        x = grid_ref[...]
        first = correlate(x, k1_ref, base, cols_in) * mask_ref[...]
        second = correlate(first, k2_ref, base, cols_out)
        smooth = second[:rows_out].astype(o_ref.dtype)
        o_ref[i] = smooth
        masked = smooth * use_ref[...]
        m_ref[i] = masked
        wide = masked.astype(jnp.float32)
        partial = wide[0:8]
        for r in range(8, rows_out, 8):
            partial = partial + wide[r : r + 8]
        lanes = partial[:, 0:LANES]
        for c in range(LANES, cols_out, LANES):
            lanes = lanes + partial[:, c : c + LANES]
        s_ref[i] = lanes
        return carry

    lax.fori_loop(0, BAND_BLOCK, one_band, 0, unroll=UNROLL)


def smooth_both(center, tb, side, mask, use, kernel_one, kernel_two):
    bands, rows_out, cols_out = center.shape
    rows_in, cols_in = mask.shape
    smem = pltpu.SMEM
    return pl.pallas_call(
        smooth_kernel,
        grid=(bands // BAND_BLOCK,),
        in_specs=[
            pl.BlockSpec(memory_space=smem),
            pl.BlockSpec(memory_space=smem),
            pl.BlockSpec((rows_in, cols_in), lambda b: (0, 0)),
            pl.BlockSpec((rows_out, cols_out), lambda b: (0, 0)),
            pl.BlockSpec((BAND_BLOCK, rows_out, cols_out), lambda b: (b, 0, 0)),
            pl.BlockSpec((BAND_BLOCK, tb.shape[1], cols_out), lambda b: (b, 0, 0)),
            pl.BlockSpec((BAND_BLOCK, rows_in, side.shape[2]), lambda b: (b, 0, 0)),
        ],
        out_specs=[
            pl.BlockSpec((BAND_BLOCK, rows_out, cols_out), lambda b: (b, 0, 0)),
            pl.BlockSpec((BAND_BLOCK, rows_out, cols_out), lambda b: (b, 0, 0)),
            pl.BlockSpec((BAND_BLOCK, 8, LANES), lambda b: (b, 0, 0)),
        ],
        out_shape=[
            jax.ShapeDtypeStruct((bands, rows_out, cols_out), jnp.bfloat16),
            jax.ShapeDtypeStruct((bands, rows_out, cols_out), jnp.bfloat16),
            jax.ShapeDtypeStruct((bands, 8, LANES), jnp.float32),
        ],
        scratch_shapes=[pltpu.VMEM((rows_in, cols_in), jnp.float32)],
    )(kernel_one.reshape(-1), kernel_two.reshape(-1), mask, use, center, tb, side)


def tree_psum(value):
    for axis in ("along", "across"):
        size = lax.axis_size(axis)
        step = 1
        while step < size:
            pairs = [(i, i ^ step) for i in range(size)]
            value = value + lax.ppermute(value, axis, pairs)
            step *= 2
    return value


def per_device(radiance, kernel_one, kernel_two, usable_mask):
    band_count, tile_rows, tile_cols = radiance.shape
    n_across = lax.axis_size("across")
    n_along = lax.axis_size("along")
    col0 = lax.axis_index("across") * tile_cols
    row0 = lax.axis_index("along") * tile_rows

    top, bottom = shift_pair(radiance, "along", 1, HALO)
    tall = jnp.concatenate([radiance, bottom, top], axis=1)
    flat_strips = [
        lax.slice_in_dim(tall, start, start + HALO, axis=2).reshape(band_count, -1)
        for start in (tile_cols - HALO, 0)
    ]
    count_across = lax.axis_size("across")
    forward = [(i, i + 1) for i in range(count_across - 1)]
    backward = [(target, source) for source, target in forward]
    left = lax.ppermute(flat_strips[0], "across", forward).reshape(band_count, -1, HALO)
    right = lax.ppermute(flat_strips[1], "across", backward).reshape(band_count, -1, HALO)
    rows_in = tall.shape[1]
    gap = LANES - 2 * HALO
    side = jnp.concatenate(
        [right, jnp.zeros((band_count, rows_in, gap), right.dtype), left], axis=2
    )
    tb = jnp.concatenate([bottom, top], axis=1)
    cols_in = tile_cols + LANES

    pos_rows = lax.broadcasted_iota(jnp.int32, (rows_in, cols_in), 0)
    pos_cols = lax.broadcasted_iota(jnp.int32, (rows_in, cols_in), 1)
    mid_rows = jnp.where(pos_rows < tile_rows + HALO, pos_rows, pos_rows - rows_in) + row0
    mid_cols = jnp.where(pos_cols < tile_cols + LANES // 2, pos_cols, pos_cols - cols_in) + col0
    inside = (
        (mid_rows >= 0)
        & (mid_rows < n_along * tile_rows)
        & (mid_cols >= 0)
        & (mid_cols < n_across * tile_cols)
    )
    mid_mask = inside.astype(jnp.float32)

    use = usable_mask.astype(jnp.bfloat16)
    smoothed, masked, partial = smooth_both(
        radiance, tb, side, mid_mask, use, kernel_one, kernel_two
    )
    flat = masked.reshape(band_count, tile_rows * tile_cols)
    local_count = jnp.sum(usable_mask.astype(jnp.float32))
    local_sum = jnp.sum(partial, axis=(1, 2))
    local_gram = lax.dot_general(
        flat, flat, (((1,), (1,)), ((), ())), preferred_element_type=jnp.float32
    )
    half = band_count // 2
    upper_a = local_gram[:half, :half]
    lower_c = local_gram[half:, half:]
    below = lax.broadcasted_iota(jnp.int32, (half, half), 0) >= lax.broadcasted_iota(
        jnp.int32, (half, half), 1
    )
    folded = jnp.where(below, upper_a, lower_c)
    extra = jnp.zeros((8, band_count), jnp.float32)
    extra = extra.at[0].set(local_sum).at[1, 0].set(local_count)
    extra = extra.at[2, :half].set(jnp.diagonal(lower_c))
    body = jnp.concatenate([local_gram[half:, :half], folded], axis=1)
    packed = tree_psum(jnp.concatenate([body, extra], axis=0))
    cross = packed[:half, :half]
    folded = packed[:half, half:]
    strict = jnp.where(below, folded, 0.0)
    strict_low = strict - jnp.diag(jnp.diagonal(folded))
    block_a = strict + strict_low.T
    strict_up = jnp.where(below, 0.0, folded)
    block_c = strict_up + strict_up.T + jnp.diag(packed[half + 2, :half])
    gram = jnp.concatenate(
        [
            jnp.concatenate([block_a, cross.T], axis=1),
            jnp.concatenate([cross, block_c], axis=1),
        ],
        axis=0,
    )
    band_sum = packed[half]
    count = packed[half + 1, 0]

    global_mean = band_sum / count
    covariance = (gram - count * jnp.outer(global_mean, global_mean)) / (count - 1.0)
    loading = 0.01 * jnp.trace(covariance) / band_count
    loaded = covariance + loading * jnp.eye(band_count, dtype=jnp.float32)
    lower = jnp.linalg.cholesky(loaded)
    whitener = lax.linalg.triangular_solve(
        lower, jnp.eye(band_count, dtype=jnp.float32), left_side=True, lower=True
    )
    centered = (
        smoothed.astype(jnp.float32).reshape(band_count, tile_rows * tile_cols)
        - global_mean[:, None]
    )
    whitened = jnp.dot(
        whitener, centered, precision=lax.Precision.HIGH, preferred_element_type=jnp.float32
    )
    distance = jnp.sum(whitened * whitened, axis=0).reshape(tile_rows, tile_cols)
    standard = (distance - band_count) / math.sqrt(2.0 * band_count)
    return standard * usable_mask.astype(jnp.float32)


def solution(mesh):
    in_specs = (P(None, "along", "across"), P(), P(), P("along", "across"))
    out_specs = P("along", "across")
    return jax.shard_map(
        per_device, mesh=mesh, in_specs=in_specs, out_specs=out_specs, check_vma=False
    )
```

```python
import math

import jax
import jax.numpy as jnp
from jax import lax
from jax.experimental import pallas as pl
from jax.experimental.pallas import tpu as pltpu
from jax.sharding import PartitionSpec as P

KSIZE = 5
REACH = KSIZE // 2
HALO = 2 * REACH
LANES = 128
BAND_BLOCK = 8
UNROLL = 2


def shift_pair(block, axis, dim, width):
    count = lax.axis_size(axis)
    forward = [(i, i + 1) for i in range(count - 1)]
    backward = [(target, source) for source, target in forward]
    low = lax.ppermute(
        lax.slice_in_dim(block, block.shape[dim] - width, None, axis=dim), axis, forward
    )
    high = lax.ppermute(lax.slice_in_dim(block, 0, width, axis=dim), axis, backward)
    return low, high


def smooth_kernel(
    k1_ref, k2_ref, mask_ref, use_ref, x_ref, tb_ref, side_ref, o_ref, m_ref, s_ref, grid_ref
):
    block = pl.program_id(0)
    rows_in, cols_in = grid_ref.shape
    rows_out, cols_out = o_ref.shape[1], o_ref.shape[2]

    def correlate(x, taps, base, cols):
        total = None
        for p in range(KSIZE):
            part = None
            for q in range(KSIZE):
                shift = (REACH - q) % cols_in
                xq = pltpu.roll(x, shift, 1) if shift else x
                term = taps[base + p * KSIZE + q] * xq[:, :cols]
                part = term if part is None else part + term
            shift = (REACH - p) % rows_in
            if shift:
                part = pltpu.roll(part, shift, 0)
            total = part if total is None else total + part
        return total

    def one_band(i, carry):
        band = block * BAND_BLOCK + i
        base = band * (KSIZE * KSIZE)
        grid_ref[:rows_out, :cols_out] = x_ref[i].astype(jnp.float32)
        grid_ref[rows_out:, :cols_out] = tb_ref[i].astype(jnp.float32)
        grid_ref[:, cols_out:] = side_ref[i].astype(jnp.float32)
        x = grid_ref[...]
        first = correlate(x, k1_ref, base, cols_in) * mask_ref[...]
        second = correlate(first, k2_ref, base, cols_out)
        smooth = second[:rows_out].astype(o_ref.dtype)
        o_ref[i] = smooth
        masked = smooth * use_ref[...]
        m_ref[i] = masked
        wide = masked.astype(jnp.float32)
        partial = wide[0:8]
        for r in range(8, rows_out, 8):
            partial = partial + wide[r : r + 8]
        lanes = partial[:, 0:LANES]
        for c in range(LANES, cols_out, LANES):
            lanes = lanes + partial[:, c : c + LANES]
        s_ref[i] = lanes
        return carry

    lax.fori_loop(0, BAND_BLOCK, one_band, 0, unroll=UNROLL)


def smooth_both(center, tb, side, mask, use, kernel_one, kernel_two):
    bands, rows_out, cols_out = center.shape
    rows_in, cols_in = mask.shape
    smem = pltpu.SMEM
    return pl.pallas_call(
        smooth_kernel,
        grid=(bands // BAND_BLOCK,),
        in_specs=[
            pl.BlockSpec(memory_space=smem),
            pl.BlockSpec(memory_space=smem),
            pl.BlockSpec((rows_in, cols_in), lambda b: (0, 0)),
            pl.BlockSpec((rows_out, cols_out), lambda b: (0, 0)),
            pl.BlockSpec((BAND_BLOCK, rows_out, cols_out), lambda b: (b, 0, 0)),
            pl.BlockSpec((BAND_BLOCK, tb.shape[1], cols_out), lambda b: (b, 0, 0)),
            pl.BlockSpec((BAND_BLOCK, rows_in, side.shape[2]), lambda b: (b, 0, 0)),
        ],
        out_specs=[
            pl.BlockSpec((BAND_BLOCK, rows_out, cols_out), lambda b: (b, 0, 0)),
            pl.BlockSpec((BAND_BLOCK, rows_out, cols_out), lambda b: (b, 0, 0)),
            pl.BlockSpec((BAND_BLOCK, 8, LANES), lambda b: (b, 0, 0)),
        ],
        out_shape=[
            jax.ShapeDtypeStruct((bands, rows_out, cols_out), jnp.bfloat16),
            jax.ShapeDtypeStruct((bands, rows_out, cols_out), jnp.bfloat16),
            jax.ShapeDtypeStruct((bands, 8, LANES), jnp.float32),
        ],
        scratch_shapes=[pltpu.VMEM((rows_in, cols_in), jnp.float32)],
    )(kernel_one.reshape(-1), kernel_two.reshape(-1), mask, use, center, tb, side)


def tree_psum(value):
    for axis in ("along", "across"):
        size = lax.axis_size(axis)
        step = 1
        while step < size:
            pairs = [(i, i ^ step) for i in range(size)]
            value = value + lax.ppermute(value, axis, pairs)
            step *= 2
    return value


def per_device(radiance, kernel_one, kernel_two, usable_mask):
    band_count, tile_rows, tile_cols = radiance.shape
    n_across = lax.axis_size("across")
    n_along = lax.axis_size("along")
    col0 = lax.axis_index("across") * tile_cols
    row0 = lax.axis_index("along") * tile_rows

    top, bottom = shift_pair(radiance, "along", 1, HALO)
    tall = jnp.concatenate([radiance, bottom, top], axis=1)
    flat_strips = [
        lax.slice_in_dim(tall, start, start + HALO, axis=2).reshape(band_count, -1)
        for start in (tile_cols - HALO, 0)
    ]
    count_across = lax.axis_size("across")
    forward = [(i, i + 1) for i in range(count_across - 1)]
    backward = [(target, source) for source, target in forward]
    left = lax.ppermute(flat_strips[0], "across", forward).reshape(band_count, -1, HALO)
    right = lax.ppermute(flat_strips[1], "across", backward).reshape(band_count, -1, HALO)
    rows_in = tall.shape[1]
    gap = LANES - 2 * HALO
    side = jnp.concatenate(
        [right, jnp.zeros((band_count, rows_in, gap), right.dtype), left], axis=2
    )
    tb = jnp.concatenate([bottom, top], axis=1)
    cols_in = tile_cols + LANES

    pos_rows = lax.broadcasted_iota(jnp.int32, (rows_in, cols_in), 0)
    pos_cols = lax.broadcasted_iota(jnp.int32, (rows_in, cols_in), 1)
    mid_rows = jnp.where(pos_rows < tile_rows + HALO, pos_rows, pos_rows - rows_in) + row0
    mid_cols = jnp.where(pos_cols < tile_cols + LANES // 2, pos_cols, pos_cols - cols_in) + col0
    inside = (
        (mid_rows >= 0)
        & (mid_rows < n_along * tile_rows)
        & (mid_cols >= 0)
        & (mid_cols < n_across * tile_cols)
    )
    mid_mask = inside.astype(jnp.float32)

    use = usable_mask.astype(jnp.bfloat16)
    smoothed, masked, partial = smooth_both(
        radiance, tb, side, mid_mask, use, kernel_one, kernel_two
    )
    flat = masked.reshape(band_count, tile_rows * tile_cols)
    local_count = jnp.sum(usable_mask.astype(jnp.float32))
    local_sum = jnp.sum(partial, axis=(1, 2))
    local_gram = lax.dot_general(
        flat, flat, (((1,), (1,)), ((), ())), preferred_element_type=jnp.float32
    )
    half = band_count // 2
    upper_a = local_gram[:half, :half]
    lower_c = local_gram[half:, half:]
    below = lax.broadcasted_iota(jnp.int32, (half, half), 0) >= lax.broadcasted_iota(
        jnp.int32, (half, half), 1
    )
    folded = jnp.where(below, upper_a, lower_c)
    extra = jnp.zeros((8, band_count), jnp.float32)
    extra = extra.at[0].set(local_sum).at[1, 0].set(local_count)
    extra = extra.at[2, :half].set(jnp.diagonal(lower_c))
    body = jnp.concatenate([local_gram[half:, :half], folded], axis=1)
    packed = tree_psum(jnp.concatenate([body, extra], axis=0))
    cross = packed[:half, :half]
    folded = packed[:half, half:]
    strict = jnp.where(below, folded, 0.0)
    strict_low = strict - jnp.diag(jnp.diagonal(folded))
    block_a = strict + strict_low.T
    strict_up = jnp.where(below, 0.0, folded)
    block_c = strict_up + strict_up.T + jnp.diag(packed[half + 2, :half])
    gram = jnp.concatenate(
        [
            jnp.concatenate([block_a, cross.T], axis=1),
            jnp.concatenate([cross, block_c], axis=1),
        ],
        axis=0,
    )
    band_sum = packed[half]
    count = packed[half + 1, 0]

    global_mean = band_sum / count
    covariance = (gram - count * jnp.outer(global_mean, global_mean)) / (count - 1.0)
    loading = 0.01 * jnp.trace(covariance) / band_count
    loaded = covariance + loading * jnp.eye(band_count, dtype=jnp.float32)
    lower = jnp.linalg.cholesky(loaded)
    centered = (
        smoothed.astype(jnp.float32).reshape(band_count, tile_rows * tile_cols)
        - global_mean[:, None]
    )
    whitened = lax.linalg.triangular_solve(lower, centered, left_side=True, lower=True)
    distance = jnp.sum(whitened * whitened, axis=0).reshape(tile_rows, tile_cols)
    standard = (distance - band_count) / math.sqrt(2.0 * band_count)
    return standard * usable_mask.astype(jnp.float32)


def solution(mesh):
    in_specs = (P(None, "along", "across"), P(), P(), P("along", "across"))
    out_specs = P("along", "across")
    return jax.shard_map(
        per_device, mesh=mesh, in_specs=in_specs, out_specs=out_specs, check_vma=False
    )
```

```python
import math

import jax
import jax.numpy as jnp
from jax import lax
from jax.experimental import pallas as pl
from jax.experimental.pallas import tpu as pltpu
from jax.sharding import PartitionSpec as P

KSIZE = 5
REACH = KSIZE // 2
HALO = 2 * REACH
LANES = 128
BAND_BLOCK = 8
UNROLL = 2


def shift_pair(block, axis, dim, width):
    count = lax.axis_size(axis)
    forward = [(i, i + 1) for i in range(count - 1)]
    backward = [(target, source) for source, target in forward]
    low = lax.ppermute(
        lax.slice_in_dim(block, block.shape[dim] - width, None, axis=dim), axis, forward
    )
    high = lax.ppermute(lax.slice_in_dim(block, 0, width, axis=dim), axis, backward)
    return low, high


def smooth_kernel(
    k1_ref, k2_ref, mask_ref, use_ref, x_ref, tb_ref, side_ref, o_ref, m_ref, s_ref, grid_ref
):
    block = pl.program_id(0)
    rows_in, cols_in = grid_ref.shape
    rows_out, cols_out = o_ref.shape[1], o_ref.shape[2]

    def correlate(x, taps, base, cols):
        total = None
        for p in range(KSIZE):
            part = None
            for q in range(KSIZE):
                shift = (REACH - q) % cols_in
                xq = pltpu.roll(x, shift, 1) if shift else x
                term = taps[base + p * KSIZE + q] * xq[:, :cols]
                part = term if part is None else part + term
            shift = (REACH - p) % rows_in
            if shift:
                part = pltpu.roll(part, shift, 0)
            total = part if total is None else total + part
        return total

    def one_band(i, carry):
        band = block * BAND_BLOCK + i
        base = band * (KSIZE * KSIZE)
        grid_ref[:rows_out, :cols_out] = x_ref[i].astype(jnp.float32)
        grid_ref[rows_out:, :cols_out] = tb_ref[i].astype(jnp.float32)
        grid_ref[:, cols_out:] = side_ref[i].astype(jnp.float32)
        x = grid_ref[...]
        first = correlate(x, k1_ref, base, cols_in) * mask_ref[...]
        second = correlate(first, k2_ref, base, cols_out)
        smooth = second[:rows_out].astype(o_ref.dtype)
        o_ref[i] = smooth
        masked = smooth * use_ref[...]
        m_ref[i] = masked
        wide = masked.astype(jnp.float32)
        partial = wide[0:8]
        for r in range(8, rows_out, 8):
            partial = partial + wide[r : r + 8]
        lanes = partial[:, 0:LANES]
        for c in range(LANES, cols_out, LANES):
            lanes = lanes + partial[:, c : c + LANES]
        s_ref[i] = lanes
        return carry

    lax.fori_loop(0, BAND_BLOCK, one_band, 0, unroll=UNROLL)


def smooth_both(center, tb, side, mask, use, kernel_one, kernel_two):
    bands, rows_out, cols_out = center.shape
    rows_in, cols_in = mask.shape
    smem = pltpu.SMEM
    return pl.pallas_call(
        smooth_kernel,
        grid=(bands // BAND_BLOCK,),
        in_specs=[
            pl.BlockSpec(memory_space=smem),
            pl.BlockSpec(memory_space=smem),
            pl.BlockSpec((rows_in, cols_in), lambda b: (0, 0)),
            pl.BlockSpec((rows_out, cols_out), lambda b: (0, 0)),
            pl.BlockSpec((BAND_BLOCK, rows_out, cols_out), lambda b: (b, 0, 0)),
            pl.BlockSpec((BAND_BLOCK, tb.shape[1], cols_out), lambda b: (b, 0, 0)),
            pl.BlockSpec((BAND_BLOCK, rows_in, side.shape[2]), lambda b: (b, 0, 0)),
        ],
        out_specs=[
            pl.BlockSpec((BAND_BLOCK, rows_out, cols_out), lambda b: (b, 0, 0)),
            pl.BlockSpec((BAND_BLOCK, rows_out, cols_out), lambda b: (b, 0, 0)),
            pl.BlockSpec((BAND_BLOCK, 8, LANES), lambda b: (b, 0, 0)),
        ],
        out_shape=[
            jax.ShapeDtypeStruct((bands, rows_out, cols_out), jnp.bfloat16),
            jax.ShapeDtypeStruct((bands, rows_out, cols_out), jnp.bfloat16),
            jax.ShapeDtypeStruct((bands, 8, LANES), jnp.float32),
        ],
        scratch_shapes=[pltpu.VMEM((rows_in, cols_in), jnp.float32)],
    )(kernel_one.reshape(-1), kernel_two.reshape(-1), mask, use, center, tb, side)


def tree_psum(value):
    for axis in ("along", "across"):
        size = lax.axis_size(axis)
        step = 1
        while step < size:
            pairs = [(i, i ^ step) for i in range(size)]
            value = value + lax.ppermute(value, axis, pairs)
            step *= 2
    return value


def lower_inverse(lower):
    size = lower.shape[0]
    half = size // 2
    eye = jnp.eye(half, dtype=lower.dtype)
    diagonal = jnp.stack([lower[:half, :half], lower[half:, half:]])
    inverses = lax.linalg.triangular_solve(
        diagonal, jnp.stack([eye, eye]), left_side=True, lower=True
    )
    top, bottom = inverses[0], inverses[1]
    high = lax.Precision.HIGHEST
    cross = -jnp.dot(bottom, jnp.dot(lower[half:, :half], top, precision=high), precision=high)
    return jnp.concatenate(
        [
            jnp.concatenate([top, jnp.zeros((half, size - half), lower.dtype)], axis=1),
            jnp.concatenate([cross, bottom], axis=1),
        ],
        axis=0,
    )


def per_device(radiance, kernel_one, kernel_two, usable_mask):
    band_count, tile_rows, tile_cols = radiance.shape
    n_across = lax.axis_size("across")
    n_along = lax.axis_size("along")
    col0 = lax.axis_index("across") * tile_cols
    row0 = lax.axis_index("along") * tile_rows

    top, bottom = shift_pair(radiance, "along", 1, HALO)
    tall = jnp.concatenate([radiance, bottom, top], axis=1)
    flat_strips = [
        lax.slice_in_dim(tall, start, start + HALO, axis=2).reshape(band_count, -1)
        for start in (tile_cols - HALO, 0)
    ]
    count_across = lax.axis_size("across")
    forward = [(i, i + 1) for i in range(count_across - 1)]
    backward = [(target, source) for source, target in forward]
    left = lax.ppermute(flat_strips[0], "across", forward).reshape(band_count, -1, HALO)
    right = lax.ppermute(flat_strips[1], "across", backward).reshape(band_count, -1, HALO)
    rows_in = tall.shape[1]
    gap = LANES - 2 * HALO
    side = jnp.concatenate(
        [right, jnp.zeros((band_count, rows_in, gap), right.dtype), left], axis=2
    )
    tb = jnp.concatenate([bottom, top], axis=1)
    cols_in = tile_cols + LANES

    pos_rows = lax.broadcasted_iota(jnp.int32, (rows_in, cols_in), 0)
    pos_cols = lax.broadcasted_iota(jnp.int32, (rows_in, cols_in), 1)
    mid_rows = jnp.where(pos_rows < tile_rows + HALO, pos_rows, pos_rows - rows_in) + row0
    mid_cols = jnp.where(pos_cols < tile_cols + LANES // 2, pos_cols, pos_cols - cols_in) + col0
    inside = (
        (mid_rows >= 0)
        & (mid_rows < n_along * tile_rows)
        & (mid_cols >= 0)
        & (mid_cols < n_across * tile_cols)
    )
    mid_mask = inside.astype(jnp.float32)

    use = usable_mask.astype(jnp.bfloat16)
    smoothed, masked, partial = smooth_both(
        radiance, tb, side, mid_mask, use, kernel_one, kernel_two
    )
    flat = masked.reshape(band_count, tile_rows * tile_cols)
    local_count = jnp.sum(usable_mask.astype(jnp.float32))
    local_sum = jnp.sum(partial, axis=(1, 2))
    local_gram = lax.dot_general(
        flat, flat, (((1,), (1,)), ((), ())), preferred_element_type=jnp.float32
    )
    half = band_count // 2
    upper_a = local_gram[:half, :half]
    lower_c = local_gram[half:, half:]
    below = lax.broadcasted_iota(jnp.int32, (half, half), 0) >= lax.broadcasted_iota(
        jnp.int32, (half, half), 1
    )
    folded = jnp.where(below, upper_a, lower_c)
    extra = jnp.zeros((8, band_count), jnp.float32)
    extra = extra.at[0].set(local_sum).at[1, 0].set(local_count)
    extra = extra.at[2, :half].set(jnp.diagonal(lower_c))
    body = jnp.concatenate([local_gram[half:, :half], folded], axis=1)
    packed = tree_psum(jnp.concatenate([body, extra], axis=0))
    cross = packed[:half, :half]
    folded = packed[:half, half:]
    strict = jnp.where(below, folded, 0.0)
    strict_low = strict - jnp.diag(jnp.diagonal(folded))
    block_a = strict + strict_low.T
    strict_up = jnp.where(below, 0.0, folded)
    block_c = strict_up + strict_up.T + jnp.diag(packed[half + 2, :half])
    gram = jnp.concatenate(
        [
            jnp.concatenate([block_a, cross.T], axis=1),
            jnp.concatenate([cross, block_c], axis=1),
        ],
        axis=0,
    )
    band_sum = packed[half]
    count = packed[half + 1, 0]

    global_mean = band_sum / count
    covariance = (gram - count * jnp.outer(global_mean, global_mean)) / (count - 1.0)
    loading = 0.01 * jnp.trace(covariance) / band_count
    loaded = covariance + loading * jnp.eye(band_count, dtype=jnp.float32)
    lower = jnp.linalg.cholesky(loaded)
    whitener = lower_inverse(lower)
    centered = (
        smoothed.astype(jnp.float32).reshape(band_count, tile_rows * tile_cols)
        - global_mean[:, None]
    )
    whitened = jnp.dot(
        whitener, centered, precision=lax.Precision.HIGH, preferred_element_type=jnp.float32
    )
    distance = jnp.sum(whitened * whitened, axis=0).reshape(tile_rows, tile_cols)
    standard = (distance - band_count) / math.sqrt(2.0 * band_count)
    return standard * usable_mask.astype(jnp.float32)


def solution(mesh):
    in_specs = (P(None, "along", "across"), P(), P(), P("along", "across"))
    out_specs = P("along", "across")
    return jax.shard_map(
        per_device, mesh=mesh, in_specs=in_specs, out_specs=out_specs, check_vma=False
    )
```

```python
import math

import jax
import jax.numpy as jnp
from jax import lax
from jax.experimental import pallas as pl
from jax.experimental.pallas import tpu as pltpu
from jax.sharding import PartitionSpec as P

KSIZE = 5
REACH = KSIZE // 2
HALO = 2 * REACH
LANES = 128
BAND_BLOCK = 8
UNROLL = 2


def shift_pair(block, axis, dim, width):
    count = lax.axis_size(axis)
    forward = [(i, i + 1) for i in range(count - 1)]
    backward = [(target, source) for source, target in forward]
    low = lax.ppermute(
        lax.slice_in_dim(block, block.shape[dim] - width, None, axis=dim), axis, forward
    )
    high = lax.ppermute(lax.slice_in_dim(block, 0, width, axis=dim), axis, backward)
    return low, high


def smooth_kernel(
    k1_ref, k2_ref, mask_ref, use_ref, x_ref, tb_ref, side_ref, o_ref, m_ref, s_ref, grid_ref
):
    block = pl.program_id(0)
    rows_in, cols_in = grid_ref.shape
    rows_out, cols_out = o_ref.shape[1], o_ref.shape[2]

    def correlate(x, taps, base, cols):
        total = None
        for p in range(KSIZE):
            part = None
            for q in range(KSIZE):
                shift = (REACH - q) % cols_in
                xq = pltpu.roll(x, shift, 1) if shift else x
                term = taps[base + p * KSIZE + q] * xq[:, :cols]
                part = term if part is None else part + term
            shift = (REACH - p) % rows_in
            if shift:
                part = pltpu.roll(part, shift, 0)
            total = part if total is None else total + part
        return total

    def one_band(i, carry):
        band = block * BAND_BLOCK + i
        base = band * (KSIZE * KSIZE)
        grid_ref[:rows_out, :cols_out] = x_ref[i].astype(jnp.float32)
        grid_ref[rows_out:, :cols_out] = tb_ref[i].astype(jnp.float32)
        grid_ref[:, cols_out:] = side_ref[i].astype(jnp.float32)
        x = grid_ref[...]
        first = correlate(x, k1_ref, base, cols_in) * mask_ref[...]
        second = correlate(first, k2_ref, base, cols_out)
        smooth = second[:rows_out].astype(o_ref.dtype)
        o_ref[i] = smooth
        masked = smooth * use_ref[...]
        m_ref[i] = masked
        wide = masked.astype(jnp.float32)
        partial = wide[0:8]
        for r in range(8, rows_out, 8):
            partial = partial + wide[r : r + 8]
        lanes = partial[:, 0:LANES]
        for c in range(LANES, cols_out, LANES):
            lanes = lanes + partial[:, c : c + LANES]
        s_ref[i] = lanes
        return carry

    lax.fori_loop(0, BAND_BLOCK, one_band, 0, unroll=UNROLL)


def smooth_both(center, tb, side, mask, use, kernel_one, kernel_two):
    bands, rows_out, cols_out = center.shape
    rows_in, cols_in = mask.shape
    smem = pltpu.SMEM
    return pl.pallas_call(
        smooth_kernel,
        grid=(bands // BAND_BLOCK,),
        in_specs=[
            pl.BlockSpec(memory_space=smem),
            pl.BlockSpec(memory_space=smem),
            pl.BlockSpec((rows_in, cols_in), lambda b: (0, 0)),
            pl.BlockSpec((rows_out, cols_out), lambda b: (0, 0)),
            pl.BlockSpec((BAND_BLOCK, rows_out, cols_out), lambda b: (b, 0, 0)),
            pl.BlockSpec((BAND_BLOCK, tb.shape[1], cols_out), lambda b: (b, 0, 0)),
            pl.BlockSpec((BAND_BLOCK, rows_in, side.shape[2]), lambda b: (b, 0, 0)),
        ],
        out_specs=[
            pl.BlockSpec((BAND_BLOCK, rows_out, cols_out), lambda b: (b, 0, 0)),
            pl.BlockSpec((BAND_BLOCK, rows_out, cols_out), lambda b: (b, 0, 0)),
            pl.BlockSpec((BAND_BLOCK, 8, LANES), lambda b: (b, 0, 0)),
        ],
        out_shape=[
            jax.ShapeDtypeStruct((bands, rows_out, cols_out), jnp.bfloat16),
            jax.ShapeDtypeStruct((bands, rows_out, cols_out), jnp.bfloat16),
            jax.ShapeDtypeStruct((bands, 8, LANES), jnp.float32),
        ],
        scratch_shapes=[pltpu.VMEM((rows_in, cols_in), jnp.float32)],
    )(kernel_one.reshape(-1), kernel_two.reshape(-1), mask, use, center, tb, side)


def tree_psum(value):
    for axis in ("along", "across"):
        size = lax.axis_size(axis)
        step = 1
        while step < size:
            pairs = [(i, i ^ step) for i in range(size)]
            value = value + lax.ppermute(value, axis, pairs)
            step *= 2
    return value


def lower_inverse(lower):
    size = lower.shape[0]
    half = size // 2
    eye = jnp.eye(half, dtype=lower.dtype)
    diagonal = jnp.stack([lower[:half, :half], lower[half:, half:]])
    inverses = lax.linalg.triangular_solve(
        diagonal, jnp.stack([eye, eye]), left_side=True, lower=True
    )
    top, bottom = inverses[0], inverses[1]
    high = lax.Precision.HIGHEST
    cross = -jnp.dot(bottom, jnp.dot(lower[half:, :half], top, precision=high), precision=high)
    return jnp.concatenate(
        [
            jnp.concatenate([top, jnp.zeros((half, size - half), lower.dtype)], axis=1),
            jnp.concatenate([cross, bottom], axis=1),
        ],
        axis=0,
    )


def per_device(radiance, kernel_one, kernel_two, usable_mask):
    band_count, tile_rows, tile_cols = radiance.shape
    n_across = lax.axis_size("across")
    n_along = lax.axis_size("along")
    col0 = lax.axis_index("across") * tile_cols
    row0 = lax.axis_index("along") * tile_rows

    top, bottom = shift_pair(radiance, "along", 1, HALO)
    tall = jnp.concatenate([radiance, bottom, top], axis=1)
    flat_strips = [
        lax.slice_in_dim(tall, start, start + HALO, axis=2).reshape(band_count, -1)
        for start in (tile_cols - HALO, 0)
    ]
    count_across = lax.axis_size("across")
    forward = [(i, i + 1) for i in range(count_across - 1)]
    backward = [(target, source) for source, target in forward]
    left = lax.ppermute(flat_strips[0], "across", forward).reshape(band_count, -1, HALO)
    right = lax.ppermute(flat_strips[1], "across", backward).reshape(band_count, -1, HALO)
    rows_in = tall.shape[1]
    gap = LANES - 2 * HALO
    side = jnp.concatenate(
        [right, jnp.zeros((band_count, rows_in, gap), right.dtype), left], axis=2
    )
    tb = jnp.concatenate([bottom, top], axis=1)
    cols_in = tile_cols + LANES

    pos_rows = lax.broadcasted_iota(jnp.int32, (rows_in, cols_in), 0)
    pos_cols = lax.broadcasted_iota(jnp.int32, (rows_in, cols_in), 1)
    mid_rows = jnp.where(pos_rows < tile_rows + HALO, pos_rows, pos_rows - rows_in) + row0
    mid_cols = jnp.where(pos_cols < tile_cols + LANES // 2, pos_cols, pos_cols - cols_in) + col0
    inside = (
        (mid_rows >= 0)
        & (mid_rows < n_along * tile_rows)
        & (mid_cols >= 0)
        & (mid_cols < n_across * tile_cols)
    )
    mid_mask = inside.astype(jnp.float32)

    use = usable_mask.astype(jnp.bfloat16)
    smoothed, masked, partial = smooth_both(
        radiance, tb, side, mid_mask, use, kernel_one, kernel_two
    )
    flat = masked.reshape(band_count, tile_rows * tile_cols)
    local_count = jnp.sum(usable_mask.astype(jnp.float32))
    local_sum = jnp.sum(partial, axis=(1, 2))
    local_gram = lax.dot_general(
        flat, flat, (((1,), (1,)), ((), ())), preferred_element_type=jnp.float32
    )
    half = band_count // 2
    upper_a = local_gram[:half, :half]
    lower_c = local_gram[half:, half:]
    rows = lax.broadcasted_iota(jnp.int32, (half, half), 0)
    cols = lax.broadcasted_iota(jnp.int32, (half, half), 1)
    below = rows >= cols
    on_diagonal = rows == cols
    folded = jnp.where(below, upper_a, lower_c)
    diagonal_c = jnp.sum(jnp.where(on_diagonal, lower_c, 0.0), axis=0)
    first_slot = lax.broadcasted_iota(jnp.int32, (band_count,), 0) == 0
    extra = jnp.concatenate(
        [
            local_sum[None],
            jnp.where(first_slot, local_count, 0.0)[None],
            jnp.concatenate([diagonal_c, jnp.zeros((band_count - half,), jnp.float32)])[None],
            jnp.zeros((5, band_count), jnp.float32),
        ],
        axis=0,
    )
    body = jnp.concatenate([local_gram[half:, :half], folded], axis=1)
    packed = tree_psum(jnp.concatenate([body, extra], axis=0))
    cross = packed[:half, :half]
    folded = packed[:half, half:]
    block_a = jnp.where(below, folded, 0.0) + jnp.where(rows > cols, folded, 0.0).T
    strict_up = jnp.where(below, 0.0, folded)
    block_c = (
        strict_up
        + strict_up.T
        + jnp.where(on_diagonal, packed[half + 2, :half][None, :], 0.0)
    )
    gram = jnp.concatenate(
        [
            jnp.concatenate([block_a, cross.T], axis=1),
            jnp.concatenate([cross, block_c], axis=1),
        ],
        axis=0,
    )
    band_sum = packed[half]
    count = packed[half + 1, 0]

    global_mean = band_sum / count
    covariance = (gram - count * jnp.outer(global_mean, global_mean)) / (count - 1.0)
    eye = jnp.eye(band_count, dtype=jnp.float32)
    loading = 0.01 * jnp.sum(jnp.where(eye > 0, covariance, 0.0)) / band_count
    loaded = covariance + loading * eye
    lower = jnp.linalg.cholesky(loaded, symmetrize_input=False)
    whitener = lower_inverse(lower)
    centered = (
        smoothed.astype(jnp.float32).reshape(band_count, tile_rows * tile_cols)
        - global_mean[:, None]
    )
    whitened = jnp.dot(
        whitener, centered, precision=lax.Precision.HIGH, preferred_element_type=jnp.float32
    )
    distance = jnp.sum(whitened * whitened, axis=0).reshape(tile_rows, tile_cols)
    standard = (distance - band_count) / math.sqrt(2.0 * band_count)
    return standard * usable_mask.astype(jnp.float32)


def solution(mesh):
    in_specs = (P(None, "along", "across"), P(), P(), P("along", "across"))
    out_specs = P("along", "across")
    return jax.shard_map(
        per_device, mesh=mesh, in_specs=in_specs, out_specs=out_specs, check_vma=False
    )
```

```python
import math

import jax
import jax.numpy as jnp
from jax import lax
from jax.experimental import pallas as pl
from jax.experimental.pallas import tpu as pltpu
from jax.sharding import PartitionSpec as P

KSIZE = 5
REACH = KSIZE // 2
HALO = 2 * REACH
LANES = 128
BAND_BLOCK = 16
UNROLL = 2


def shift_pair(block, axis, dim, width):
    count = lax.axis_size(axis)
    forward = [(i, i + 1) for i in range(count - 1)]
    backward = [(target, source) for source, target in forward]
    low = lax.ppermute(
        lax.slice_in_dim(block, block.shape[dim] - width, None, axis=dim), axis, forward
    )
    high = lax.ppermute(lax.slice_in_dim(block, 0, width, axis=dim), axis, backward)
    return low, high


def smooth_kernel(
    k1_ref, k2_ref, mask_ref, use_ref, x_ref, tb_ref, side_ref, o_ref, m_ref, s_ref, grid_ref
):
    block = pl.program_id(0)
    rows_in, cols_in = grid_ref.shape
    rows_out, cols_out = o_ref.shape[1], o_ref.shape[2]

    def correlate(x, taps, base, cols):
        total = None
        for p in range(KSIZE):
            part = None
            for q in range(KSIZE):
                shift = (REACH - q) % cols_in
                xq = pltpu.roll(x, shift, 1) if shift else x
                term = taps[base + p * KSIZE + q] * xq[:, :cols]
                part = term if part is None else part + term
            shift = (REACH - p) % rows_in
            if shift:
                part = pltpu.roll(part, shift, 0)
            total = part if total is None else total + part
        return total

    def one_band(i, carry):
        band = block * BAND_BLOCK + i
        base = band * (KSIZE * KSIZE)
        grid_ref[:rows_out, :cols_out] = x_ref[i].astype(jnp.float32)
        grid_ref[rows_out:, :cols_out] = tb_ref[i].astype(jnp.float32)
        grid_ref[:, cols_out:] = side_ref[i].astype(jnp.float32)
        x = grid_ref[...]
        first = correlate(x, k1_ref, base, cols_in) * mask_ref[...]
        second = correlate(first, k2_ref, base, cols_out)
        smooth = second[:rows_out].astype(o_ref.dtype)
        o_ref[i] = smooth
        masked = smooth * use_ref[...]
        m_ref[i] = masked
        wide = masked.astype(jnp.float32)
        partial = wide[0:8]
        for r in range(8, rows_out, 8):
            partial = partial + wide[r : r + 8]
        lanes = partial[:, 0:LANES]
        for c in range(LANES, cols_out, LANES):
            lanes = lanes + partial[:, c : c + LANES]
        s_ref[i] = lanes
        return carry

    lax.fori_loop(0, BAND_BLOCK, one_band, 0, unroll=UNROLL)


def smooth_both(center, tb, side, mask, use, kernel_one, kernel_two):
    bands, rows_out, cols_out = center.shape
    rows_in, cols_in = mask.shape
    smem = pltpu.SMEM
    return pl.pallas_call(
        smooth_kernel,
        grid=(bands // BAND_BLOCK,),
        in_specs=[
            pl.BlockSpec(memory_space=smem),
            pl.BlockSpec(memory_space=smem),
            pl.BlockSpec((rows_in, cols_in), lambda b: (0, 0)),
            pl.BlockSpec((rows_out, cols_out), lambda b: (0, 0)),
            pl.BlockSpec((BAND_BLOCK, rows_out, cols_out), lambda b: (b, 0, 0)),
            pl.BlockSpec((BAND_BLOCK, tb.shape[1], cols_out), lambda b: (b, 0, 0)),
            pl.BlockSpec((BAND_BLOCK, rows_in, side.shape[2]), lambda b: (b, 0, 0)),
        ],
        out_specs=[
            pl.BlockSpec((BAND_BLOCK, rows_out, cols_out), lambda b: (b, 0, 0)),
            pl.BlockSpec((BAND_BLOCK, rows_out, cols_out), lambda b: (b, 0, 0)),
            pl.BlockSpec((BAND_BLOCK, 8, LANES), lambda b: (b, 0, 0)),
        ],
        out_shape=[
            jax.ShapeDtypeStruct((bands, rows_out, cols_out), jnp.bfloat16),
            jax.ShapeDtypeStruct((bands, rows_out, cols_out), jnp.bfloat16),
            jax.ShapeDtypeStruct((bands, 8, LANES), jnp.float32),
        ],
        scratch_shapes=[pltpu.VMEM((rows_in, cols_in), jnp.float32)],
    )(kernel_one.reshape(-1), kernel_two.reshape(-1), mask, use, center, tb, side)


def tree_psum(value):
    for axis in ("along", "across"):
        size = lax.axis_size(axis)
        step = 1
        while step < size:
            pairs = [(i, i ^ step) for i in range(size)]
            value = value + lax.ppermute(value, axis, pairs)
            step *= 2
    return value


def lower_inverse(lower):
    size = lower.shape[0]
    half = size // 2
    eye = jnp.eye(half, dtype=lower.dtype)
    diagonal = jnp.stack([lower[:half, :half], lower[half:, half:]])
    inverses = lax.linalg.triangular_solve(
        diagonal, jnp.stack([eye, eye]), left_side=True, lower=True
    )
    top, bottom = inverses[0], inverses[1]
    high = lax.Precision.HIGHEST
    cross = -jnp.dot(bottom, jnp.dot(lower[half:, :half], top, precision=high), precision=high)
    return jnp.concatenate(
        [
            jnp.concatenate([top, jnp.zeros((half, size - half), lower.dtype)], axis=1),
            jnp.concatenate([cross, bottom], axis=1),
        ],
        axis=0,
    )


def per_device(radiance, kernel_one, kernel_two, usable_mask):
    band_count, tile_rows, tile_cols = radiance.shape
    n_across = lax.axis_size("across")
    n_along = lax.axis_size("along")
    col0 = lax.axis_index("across") * tile_cols
    row0 = lax.axis_index("along") * tile_rows

    top, bottom = shift_pair(radiance, "along", 1, HALO)
    tall = jnp.concatenate([radiance, bottom, top], axis=1)
    flat_strips = [
        lax.slice_in_dim(tall, start, start + HALO, axis=2).reshape(band_count, -1)
        for start in (tile_cols - HALO, 0)
    ]
    count_across = lax.axis_size("across")
    forward = [(i, i + 1) for i in range(count_across - 1)]
    backward = [(target, source) for source, target in forward]
    left = lax.ppermute(flat_strips[0], "across", forward).reshape(band_count, -1, HALO)
    right = lax.ppermute(flat_strips[1], "across", backward).reshape(band_count, -1, HALO)
    rows_in = tall.shape[1]
    gap = LANES - 2 * HALO
    side = jnp.concatenate(
        [right, jnp.zeros((band_count, rows_in, gap), right.dtype), left], axis=2
    )
    tb = jnp.concatenate([bottom, top], axis=1)
    cols_in = tile_cols + LANES

    pos_rows = lax.broadcasted_iota(jnp.int32, (rows_in, cols_in), 0)
    pos_cols = lax.broadcasted_iota(jnp.int32, (rows_in, cols_in), 1)
    mid_rows = jnp.where(pos_rows < tile_rows + HALO, pos_rows, pos_rows - rows_in) + row0
    mid_cols = jnp.where(pos_cols < tile_cols + LANES // 2, pos_cols, pos_cols - cols_in) + col0
    inside = (
        (mid_rows >= 0)
        & (mid_rows < n_along * tile_rows)
        & (mid_cols >= 0)
        & (mid_cols < n_across * tile_cols)
    )
    mid_mask = inside.astype(jnp.float32)

    use = usable_mask.astype(jnp.bfloat16)
    smoothed, masked, partial = smooth_both(
        radiance, tb, side, mid_mask, use, kernel_one, kernel_two
    )
    flat = masked.reshape(band_count, tile_rows * tile_cols)
    local_count = jnp.sum(usable_mask.astype(jnp.float32))
    local_sum = jnp.sum(partial, axis=(1, 2))
    local_gram = lax.dot_general(
        flat, flat, (((1,), (1,)), ((), ())), preferred_element_type=jnp.float32
    )
    half = band_count // 2
    upper_a = local_gram[:half, :half]
    lower_c = local_gram[half:, half:]
    rows = lax.broadcasted_iota(jnp.int32, (half, half), 0)
    cols = lax.broadcasted_iota(jnp.int32, (half, half), 1)
    below = rows >= cols
    on_diagonal = rows == cols
    folded = jnp.where(below, upper_a, lower_c)
    diagonal_c = jnp.sum(jnp.where(on_diagonal, lower_c, 0.0), axis=0)
    first_slot = lax.broadcasted_iota(jnp.int32, (band_count,), 0) == 0
    extra = jnp.concatenate(
        [
            local_sum[None],
            jnp.where(first_slot, local_count, 0.0)[None],
            jnp.concatenate([diagonal_c, jnp.zeros((band_count - half,), jnp.float32)])[None],
            jnp.zeros((5, band_count), jnp.float32),
        ],
        axis=0,
    )
    body = jnp.concatenate([local_gram[half:, :half], folded], axis=1)
    packed = tree_psum(jnp.concatenate([body, extra], axis=0))
    cross = packed[:half, :half]
    folded = packed[:half, half:]
    block_a = jnp.where(below, folded, 0.0) + jnp.where(rows > cols, folded, 0.0).T
    strict_up = jnp.where(below, 0.0, folded)
    block_c = (
        strict_up
        + strict_up.T
        + jnp.where(on_diagonal, packed[half + 2, :half][None, :], 0.0)
    )
    gram = jnp.concatenate(
        [
            jnp.concatenate([block_a, cross.T], axis=1),
            jnp.concatenate([cross, block_c], axis=1),
        ],
        axis=0,
    )
    band_sum = packed[half]
    count = packed[half + 1, 0]

    global_mean = band_sum / count
    covariance = (gram - count * jnp.outer(global_mean, global_mean)) / (count - 1.0)
    eye = jnp.eye(band_count, dtype=jnp.float32)
    loading = 0.01 * jnp.sum(jnp.where(eye > 0, covariance, 0.0)) / band_count
    loaded = covariance + loading * eye
    lower = jnp.linalg.cholesky(loaded, symmetrize_input=False)
    whitener = lower_inverse(lower)
    centered = (
        smoothed.astype(jnp.float32).reshape(band_count, tile_rows * tile_cols)
        - global_mean[:, None]
    )
    whitened = jnp.dot(
        whitener, centered, precision=lax.Precision.HIGH, preferred_element_type=jnp.float32
    )
    distance = jnp.sum(whitened * whitened, axis=0).reshape(tile_rows, tile_cols)
    standard = (distance - band_count) / math.sqrt(2.0 * band_count)
    return standard * usable_mask.astype(jnp.float32)


def solution(mesh):
    in_specs = (P(None, "along", "across"), P(), P(), P("along", "across"))
    out_specs = P("along", "across")
    return jax.shard_map(
        per_device, mesh=mesh, in_specs=in_specs, out_specs=out_specs, check_vma=False
    )
```

```python
import math

import jax
import jax.numpy as jnp
from jax import lax
from jax.experimental import pallas as pl
from jax.experimental.pallas import tpu as pltpu
from jax.sharding import PartitionSpec as P

KSIZE = 5
REACH = KSIZE // 2
HALO = 2 * REACH
LANES = 128
BAND_BLOCK = 16
UNROLL = 4


def shift_pair(block, axis, dim, width):
    count = lax.axis_size(axis)
    forward = [(i, i + 1) for i in range(count - 1)]
    backward = [(target, source) for source, target in forward]
    low = lax.ppermute(
        lax.slice_in_dim(block, block.shape[dim] - width, None, axis=dim), axis, forward
    )
    high = lax.ppermute(lax.slice_in_dim(block, 0, width, axis=dim), axis, backward)
    return low, high


def smooth_kernel(
    k1_ref, k2_ref, mask_ref, use_ref, x_ref, tb_ref, side_ref, o_ref, m_ref, s_ref, grid_ref
):
    block = pl.program_id(0)
    rows_in, cols_in = grid_ref.shape
    rows_out, cols_out = o_ref.shape[1], o_ref.shape[2]

    def correlate(x, taps, base, cols):
        total = None
        for p in range(KSIZE):
            part = None
            for q in range(KSIZE):
                shift = (REACH - q) % cols_in
                xq = pltpu.roll(x, shift, 1) if shift else x
                term = taps[base + p * KSIZE + q] * xq[:, :cols]
                part = term if part is None else part + term
            shift = (REACH - p) % rows_in
            if shift:
                part = pltpu.roll(part, shift, 0)
            total = part if total is None else total + part
        return total

    def one_band(i, carry):
        band = block * BAND_BLOCK + i
        base = band * (KSIZE * KSIZE)
        grid_ref[:rows_out, :cols_out] = x_ref[i].astype(jnp.float32)
        grid_ref[rows_out:, :cols_out] = tb_ref[i].astype(jnp.float32)
        grid_ref[:, cols_out:] = side_ref[i].astype(jnp.float32)
        x = grid_ref[...]
        first = correlate(x, k1_ref, base, cols_in) * mask_ref[...]
        second = correlate(first, k2_ref, base, cols_out)
        smooth = second[:rows_out].astype(o_ref.dtype)
        o_ref[i] = smooth
        masked = smooth * use_ref[...]
        m_ref[i] = masked
        wide = masked.astype(jnp.float32)
        partial = wide[0:8]
        for r in range(8, rows_out, 8):
            partial = partial + wide[r : r + 8]
        lanes = partial[:, 0:LANES]
        for c in range(LANES, cols_out, LANES):
            lanes = lanes + partial[:, c : c + LANES]
        s_ref[i] = lanes
        return carry

    lax.fori_loop(0, BAND_BLOCK, one_band, 0, unroll=UNROLL)


def smooth_both(center, tb, side, mask, use, kernel_one, kernel_two):
    bands, rows_out, cols_out = center.shape
    rows_in, cols_in = mask.shape
    smem = pltpu.SMEM
    return pl.pallas_call(
        smooth_kernel,
        grid=(bands // BAND_BLOCK,),
        in_specs=[
            pl.BlockSpec(memory_space=smem),
            pl.BlockSpec(memory_space=smem),
            pl.BlockSpec((rows_in, cols_in), lambda b: (0, 0)),
            pl.BlockSpec((rows_out, cols_out), lambda b: (0, 0)),
            pl.BlockSpec((BAND_BLOCK, rows_out, cols_out), lambda b: (b, 0, 0)),
            pl.BlockSpec((BAND_BLOCK, tb.shape[1], cols_out), lambda b: (b, 0, 0)),
            pl.BlockSpec((BAND_BLOCK, rows_in, side.shape[2]), lambda b: (b, 0, 0)),
        ],
        out_specs=[
            pl.BlockSpec((BAND_BLOCK, rows_out, cols_out), lambda b: (b, 0, 0)),
            pl.BlockSpec((BAND_BLOCK, rows_out, cols_out), lambda b: (b, 0, 0)),
            pl.BlockSpec((BAND_BLOCK, 8, LANES), lambda b: (b, 0, 0)),
        ],
        out_shape=[
            jax.ShapeDtypeStruct((bands, rows_out, cols_out), jnp.bfloat16),
            jax.ShapeDtypeStruct((bands, rows_out, cols_out), jnp.bfloat16),
            jax.ShapeDtypeStruct((bands, 8, LANES), jnp.float32),
        ],
        scratch_shapes=[pltpu.VMEM((rows_in, cols_in), jnp.float32)],
    )(kernel_one.reshape(-1), kernel_two.reshape(-1), mask, use, center, tb, side)


def tree_psum(value):
    for axis in ("along", "across"):
        size = lax.axis_size(axis)
        step = 1
        while step < size:
            pairs = [(i, i ^ step) for i in range(size)]
            value = value + lax.ppermute(value, axis, pairs)
            step *= 2
    return value


def lower_inverse(lower):
    size = lower.shape[0]
    half = size // 2
    eye = jnp.eye(half, dtype=lower.dtype)
    diagonal = jnp.stack([lower[:half, :half], lower[half:, half:]])
    inverses = lax.linalg.triangular_solve(
        diagonal, jnp.stack([eye, eye]), left_side=True, lower=True
    )
    top, bottom = inverses[0], inverses[1]
    high = lax.Precision.HIGHEST
    cross = -jnp.dot(bottom, jnp.dot(lower[half:, :half], top, precision=high), precision=high)
    return jnp.concatenate(
        [
            jnp.concatenate([top, jnp.zeros((half, size - half), lower.dtype)], axis=1),
            jnp.concatenate([cross, bottom], axis=1),
        ],
        axis=0,
    )


def per_device(radiance, kernel_one, kernel_two, usable_mask):
    band_count, tile_rows, tile_cols = radiance.shape
    n_across = lax.axis_size("across")
    n_along = lax.axis_size("along")
    col0 = lax.axis_index("across") * tile_cols
    row0 = lax.axis_index("along") * tile_rows

    top, bottom = shift_pair(radiance, "along", 1, HALO)
    tall = jnp.concatenate([radiance, bottom, top], axis=1)
    flat_strips = [
        lax.slice_in_dim(tall, start, start + HALO, axis=2).reshape(band_count, -1)
        for start in (tile_cols - HALO, 0)
    ]
    count_across = lax.axis_size("across")
    forward = [(i, i + 1) for i in range(count_across - 1)]
    backward = [(target, source) for source, target in forward]
    left = lax.ppermute(flat_strips[0], "across", forward).reshape(band_count, -1, HALO)
    right = lax.ppermute(flat_strips[1], "across", backward).reshape(band_count, -1, HALO)
    rows_in = tall.shape[1]
    gap = LANES - 2 * HALO
    side = jnp.concatenate(
        [right, jnp.zeros((band_count, rows_in, gap), right.dtype), left], axis=2
    )
    tb = jnp.concatenate([bottom, top], axis=1)
    cols_in = tile_cols + LANES

    pos_rows = lax.broadcasted_iota(jnp.int32, (rows_in, cols_in), 0)
    pos_cols = lax.broadcasted_iota(jnp.int32, (rows_in, cols_in), 1)
    mid_rows = jnp.where(pos_rows < tile_rows + HALO, pos_rows, pos_rows - rows_in) + row0
    mid_cols = jnp.where(pos_cols < tile_cols + LANES // 2, pos_cols, pos_cols - cols_in) + col0
    inside = (
        (mid_rows >= 0)
        & (mid_rows < n_along * tile_rows)
        & (mid_cols >= 0)
        & (mid_cols < n_across * tile_cols)
    )
    mid_mask = inside.astype(jnp.float32)

    use = usable_mask.astype(jnp.bfloat16)
    smoothed, masked, partial = smooth_both(
        radiance, tb, side, mid_mask, use, kernel_one, kernel_two
    )
    flat = masked.reshape(band_count, tile_rows * tile_cols)
    local_count = jnp.sum(usable_mask.astype(jnp.float32))
    local_sum = jnp.sum(partial, axis=(1, 2))
    local_gram = lax.dot_general(
        flat, flat, (((1,), (1,)), ((), ())), preferred_element_type=jnp.float32
    )
    half = band_count // 2
    upper_a = local_gram[:half, :half]
    lower_c = local_gram[half:, half:]
    rows = lax.broadcasted_iota(jnp.int32, (half, half), 0)
    cols = lax.broadcasted_iota(jnp.int32, (half, half), 1)
    below = rows >= cols
    on_diagonal = rows == cols
    folded = jnp.where(below, upper_a, lower_c)
    diagonal_c = jnp.sum(jnp.where(on_diagonal, lower_c, 0.0), axis=0)
    first_slot = lax.broadcasted_iota(jnp.int32, (band_count,), 0) == 0
    extra = jnp.concatenate(
        [
            local_sum[None],
            jnp.where(first_slot, local_count, 0.0)[None],
            jnp.concatenate([diagonal_c, jnp.zeros((band_count - half,), jnp.float32)])[None],
            jnp.zeros((5, band_count), jnp.float32),
        ],
        axis=0,
    )
    body = jnp.concatenate([local_gram[half:, :half], folded], axis=1)
    packed = tree_psum(jnp.concatenate([body, extra], axis=0))
    cross = packed[:half, :half]
    folded = packed[:half, half:]
    block_a = jnp.where(below, folded, 0.0) + jnp.where(rows > cols, folded, 0.0).T
    strict_up = jnp.where(below, 0.0, folded)
    block_c = (
        strict_up
        + strict_up.T
        + jnp.where(on_diagonal, packed[half + 2, :half][None, :], 0.0)
    )
    gram = jnp.concatenate(
        [
            jnp.concatenate([block_a, cross.T], axis=1),
            jnp.concatenate([cross, block_c], axis=1),
        ],
        axis=0,
    )
    band_sum = packed[half]
    count = packed[half + 1, 0]

    global_mean = band_sum / count
    covariance = (gram - count * jnp.outer(global_mean, global_mean)) / (count - 1.0)
    eye = jnp.eye(band_count, dtype=jnp.float32)
    loading = 0.01 * jnp.sum(jnp.where(eye > 0, covariance, 0.0)) / band_count
    loaded = covariance + loading * eye
    lower = jnp.linalg.cholesky(loaded, symmetrize_input=False)
    whitener = lower_inverse(lower)
    centered = (
        smoothed.astype(jnp.float32).reshape(band_count, tile_rows * tile_cols)
        - global_mean[:, None]
    )
    whitened = jnp.dot(
        whitener, centered, precision=lax.Precision.HIGH, preferred_element_type=jnp.float32
    )
    distance = jnp.sum(whitened * whitened, axis=0).reshape(tile_rows, tile_cols)
    standard = (distance - band_count) / math.sqrt(2.0 * band_count)
    return standard * usable_mask.astype(jnp.float32)


def solution(mesh):
    in_specs = (P(None, "along", "across"), P(), P(), P("along", "across"))
    out_specs = P("along", "across")
    return jax.shard_map(
        per_device, mesh=mesh, in_specs=in_specs, out_specs=out_specs, check_vma=False
    )
```

```python
import math

import jax
import jax.numpy as jnp
from jax import lax
from jax.experimental import pallas as pl
from jax.experimental.pallas import tpu as pltpu
from jax.sharding import PartitionSpec as P

KSIZE = 5
REACH = KSIZE // 2
HALO = 2 * REACH
LANES = 128
BAND_BLOCK = 16
UNROLL = 8


def shift_pair(block, axis, dim, width):
    count = lax.axis_size(axis)
    forward = [(i, i + 1) for i in range(count - 1)]
    backward = [(target, source) for source, target in forward]
    low = lax.ppermute(
        lax.slice_in_dim(block, block.shape[dim] - width, None, axis=dim), axis, forward
    )
    high = lax.ppermute(lax.slice_in_dim(block, 0, width, axis=dim), axis, backward)
    return low, high


def smooth_kernel(
    k1_ref, k2_ref, mask_ref, use_ref, x_ref, tb_ref, side_ref, o_ref, m_ref, s_ref, grid_ref
):
    block = pl.program_id(0)
    rows_in, cols_in = grid_ref.shape
    rows_out, cols_out = o_ref.shape[1], o_ref.shape[2]

    def correlate(x, taps, base, cols):
        total = None
        for p in range(KSIZE):
            part = None
            for q in range(KSIZE):
                shift = (REACH - q) % cols_in
                xq = pltpu.roll(x, shift, 1) if shift else x
                term = taps[base + p * KSIZE + q] * xq[:, :cols]
                part = term if part is None else part + term
            shift = (REACH - p) % rows_in
            if shift:
                part = pltpu.roll(part, shift, 0)
            total = part if total is None else total + part
        return total

    def one_band(i, carry):
        band = block * BAND_BLOCK + i
        base = band * (KSIZE * KSIZE)
        grid_ref[:rows_out, :cols_out] = x_ref[i].astype(jnp.float32)
        grid_ref[rows_out:, :cols_out] = tb_ref[i].astype(jnp.float32)
        grid_ref[:, cols_out:] = side_ref[i].astype(jnp.float32)
        x = grid_ref[...]
        first = correlate(x, k1_ref, base, cols_in) * mask_ref[...]
        second = correlate(first, k2_ref, base, cols_out)
        smooth = second[:rows_out].astype(o_ref.dtype)
        o_ref[i] = smooth
        masked = smooth * use_ref[...]
        m_ref[i] = masked
        wide = masked.astype(jnp.float32)
        partial = wide[0:8]
        for r in range(8, rows_out, 8):
            partial = partial + wide[r : r + 8]
        lanes = partial[:, 0:LANES]
        for c in range(LANES, cols_out, LANES):
            lanes = lanes + partial[:, c : c + LANES]
        s_ref[i] = lanes
        return carry

    lax.fori_loop(0, BAND_BLOCK, one_band, 0, unroll=UNROLL)


def smooth_both(center, tb, side, mask, use, kernel_one, kernel_two):
    bands, rows_out, cols_out = center.shape
    rows_in, cols_in = mask.shape
    smem = pltpu.SMEM
    return pl.pallas_call(
        smooth_kernel,
        grid=(bands // BAND_BLOCK,),
        in_specs=[
            pl.BlockSpec(memory_space=smem),
            pl.BlockSpec(memory_space=smem),
            pl.BlockSpec((rows_in, cols_in), lambda b: (0, 0)),
            pl.BlockSpec((rows_out, cols_out), lambda b: (0, 0)),
            pl.BlockSpec((BAND_BLOCK, rows_out, cols_out), lambda b: (b, 0, 0)),
            pl.BlockSpec((BAND_BLOCK, tb.shape[1], cols_out), lambda b: (b, 0, 0)),
            pl.BlockSpec((BAND_BLOCK, rows_in, side.shape[2]), lambda b: (b, 0, 0)),
        ],
        out_specs=[
            pl.BlockSpec((BAND_BLOCK, rows_out, cols_out), lambda b: (b, 0, 0)),
            pl.BlockSpec((BAND_BLOCK, rows_out, cols_out), lambda b: (b, 0, 0)),
            pl.BlockSpec((BAND_BLOCK, 8, LANES), lambda b: (b, 0, 0)),
        ],
        out_shape=[
            jax.ShapeDtypeStruct((bands, rows_out, cols_out), jnp.bfloat16),
            jax.ShapeDtypeStruct((bands, rows_out, cols_out), jnp.bfloat16),
            jax.ShapeDtypeStruct((bands, 8, LANES), jnp.float32),
        ],
        scratch_shapes=[pltpu.VMEM((rows_in, cols_in), jnp.float32)],
    )(kernel_one.reshape(-1), kernel_two.reshape(-1), mask, use, center, tb, side)


def tree_psum(value):
    for axis in ("along", "across"):
        size = lax.axis_size(axis)
        step = 1
        while step < size:
            pairs = [(i, i ^ step) for i in range(size)]
            value = value + lax.ppermute(value, axis, pairs)
            step *= 2
    return value


def lower_inverse(lower):
    size = lower.shape[0]
    half = size // 2
    eye = jnp.eye(half, dtype=lower.dtype)
    diagonal = jnp.stack([lower[:half, :half], lower[half:, half:]])
    inverses = lax.linalg.triangular_solve(
        diagonal, jnp.stack([eye, eye]), left_side=True, lower=True
    )
    top, bottom = inverses[0], inverses[1]
    high = lax.Precision.HIGHEST
    cross = -jnp.dot(bottom, jnp.dot(lower[half:, :half], top, precision=high), precision=high)
    return jnp.concatenate(
        [
            jnp.concatenate([top, jnp.zeros((half, size - half), lower.dtype)], axis=1),
            jnp.concatenate([cross, bottom], axis=1),
        ],
        axis=0,
    )


def per_device(radiance, kernel_one, kernel_two, usable_mask):
    band_count, tile_rows, tile_cols = radiance.shape
    n_across = lax.axis_size("across")
    n_along = lax.axis_size("along")
    col0 = lax.axis_index("across") * tile_cols
    row0 = lax.axis_index("along") * tile_rows

    top, bottom = shift_pair(radiance, "along", 1, HALO)
    tall = jnp.concatenate([radiance, bottom, top], axis=1)
    flat_strips = [
        lax.slice_in_dim(tall, start, start + HALO, axis=2).reshape(band_count, -1)
        for start in (tile_cols - HALO, 0)
    ]
    count_across = lax.axis_size("across")
    forward = [(i, i + 1) for i in range(count_across - 1)]
    backward = [(target, source) for source, target in forward]
    left = lax.ppermute(flat_strips[0], "across", forward).reshape(band_count, -1, HALO)
    right = lax.ppermute(flat_strips[1], "across", backward).reshape(band_count, -1, HALO)
    rows_in = tall.shape[1]
    gap = LANES - 2 * HALO
    side = jnp.concatenate(
        [right, jnp.zeros((band_count, rows_in, gap), right.dtype), left], axis=2
    )
    tb = jnp.concatenate([bottom, top], axis=1)
    cols_in = tile_cols + LANES

    pos_rows = lax.broadcasted_iota(jnp.int32, (rows_in, cols_in), 0)
    pos_cols = lax.broadcasted_iota(jnp.int32, (rows_in, cols_in), 1)
    mid_rows = jnp.where(pos_rows < tile_rows + HALO, pos_rows, pos_rows - rows_in) + row0
    mid_cols = jnp.where(pos_cols < tile_cols + LANES // 2, pos_cols, pos_cols - cols_in) + col0
    inside = (
        (mid_rows >= 0)
        & (mid_rows < n_along * tile_rows)
        & (mid_cols >= 0)
        & (mid_cols < n_across * tile_cols)
    )
    mid_mask = inside.astype(jnp.float32)

    use = usable_mask.astype(jnp.bfloat16)
    smoothed, masked, partial = smooth_both(
        radiance, tb, side, mid_mask, use, kernel_one, kernel_two
    )
    flat = masked.reshape(band_count, tile_rows * tile_cols)
    local_count = jnp.sum(usable_mask.astype(jnp.float32))
    local_sum = jnp.sum(partial, axis=(1, 2))
    local_gram = lax.dot_general(
        flat, flat, (((1,), (1,)), ((), ())), preferred_element_type=jnp.float32
    )
    half = band_count // 2
    upper_a = local_gram[:half, :half]
    lower_c = local_gram[half:, half:]
    rows = lax.broadcasted_iota(jnp.int32, (half, half), 0)
    cols = lax.broadcasted_iota(jnp.int32, (half, half), 1)
    below = rows >= cols
    on_diagonal = rows == cols
    folded = jnp.where(below, upper_a, lower_c)
    diagonal_c = jnp.sum(jnp.where(on_diagonal, lower_c, 0.0), axis=0)
    first_slot = lax.broadcasted_iota(jnp.int32, (band_count,), 0) == 0
    extra = jnp.concatenate(
        [
            local_sum[None],
            jnp.where(first_slot, local_count, 0.0)[None],
            jnp.concatenate([diagonal_c, jnp.zeros((band_count - half,), jnp.float32)])[None],
            jnp.zeros((5, band_count), jnp.float32),
        ],
        axis=0,
    )
    body = jnp.concatenate([local_gram[half:, :half], folded], axis=1)
    packed = tree_psum(jnp.concatenate([body, extra], axis=0))
    cross = packed[:half, :half]
    folded = packed[:half, half:]
    block_a = jnp.where(below, folded, 0.0) + jnp.where(rows > cols, folded, 0.0).T
    strict_up = jnp.where(below, 0.0, folded)
    block_c = (
        strict_up
        + strict_up.T
        + jnp.where(on_diagonal, packed[half + 2, :half][None, :], 0.0)
    )
    gram = jnp.concatenate(
        [
            jnp.concatenate([block_a, cross.T], axis=1),
            jnp.concatenate([cross, block_c], axis=1),
        ],
        axis=0,
    )
    band_sum = packed[half]
    count = packed[half + 1, 0]

    global_mean = band_sum / count
    covariance = (gram - count * jnp.outer(global_mean, global_mean)) / (count - 1.0)
    eye = jnp.eye(band_count, dtype=jnp.float32)
    loading = 0.01 * jnp.sum(jnp.where(eye > 0, covariance, 0.0)) / band_count
    loaded = covariance + loading * eye
    lower = jnp.linalg.cholesky(loaded, symmetrize_input=False)
    whitener = lower_inverse(lower)
    centered = (
        smoothed.astype(jnp.float32).reshape(band_count, tile_rows * tile_cols)
        - global_mean[:, None]
    )
    whitened = jnp.dot(
        whitener, centered, precision=lax.Precision.HIGH, preferred_element_type=jnp.float32
    )
    distance = jnp.sum(whitened * whitened, axis=0).reshape(tile_rows, tile_cols)
    standard = (distance - band_count) / math.sqrt(2.0 * band_count)
    return standard * usable_mask.astype(jnp.float32)


def solution(mesh):
    in_specs = (P(None, "along", "across"), P(), P(), P("along", "across"))
    out_specs = P("along", "across")
    return jax.shard_map(
        per_device, mesh=mesh, in_specs=in_specs, out_specs=out_specs, check_vma=False
    )
```

```python
import math

import jax
import jax.numpy as jnp
from jax import lax
from jax.experimental import pallas as pl
from jax.experimental.pallas import tpu as pltpu
from jax.sharding import PartitionSpec as P

KSIZE = 5
REACH = KSIZE // 2
HALO = 2 * REACH
LANES = 128
BAND_BLOCK = 8
UNROLL = 4


def shift_pair(block, axis, dim, width):
    count = lax.axis_size(axis)
    forward = [(i, i + 1) for i in range(count - 1)]
    backward = [(target, source) for source, target in forward]
    low = lax.ppermute(
        lax.slice_in_dim(block, block.shape[dim] - width, None, axis=dim), axis, forward
    )
    high = lax.ppermute(lax.slice_in_dim(block, 0, width, axis=dim), axis, backward)
    return low, high


def smooth_kernel(
    k1_ref, k2_ref, mask_ref, use_ref, x_ref, tb_ref, side_ref, o_ref, m_ref, s_ref, grid_ref
):
    block = pl.program_id(0)
    rows_in, cols_in = grid_ref.shape
    rows_out, cols_out = o_ref.shape[1], o_ref.shape[2]

    def correlate(x, taps, base, cols):
        total = None
        for p in range(KSIZE):
            part = None
            for q in range(KSIZE):
                shift = (REACH - q) % cols_in
                xq = pltpu.roll(x, shift, 1) if shift else x
                term = taps[base + p * KSIZE + q] * xq[:, :cols]
                part = term if part is None else part + term
            shift = (REACH - p) % rows_in
            if shift:
                part = pltpu.roll(part, shift, 0)
            total = part if total is None else total + part
        return total

    def one_band(i, carry):
        band = block * BAND_BLOCK + i
        base = band * (KSIZE * KSIZE)
        grid_ref[:rows_out, :cols_out] = x_ref[i].astype(jnp.float32)
        grid_ref[rows_out:, :cols_out] = tb_ref[i].astype(jnp.float32)
        grid_ref[:, cols_out:] = side_ref[i].astype(jnp.float32)
        x = grid_ref[...]
        first = correlate(x, k1_ref, base, cols_in) * mask_ref[...]
        second = correlate(first, k2_ref, base, cols_out)
        smooth = second[:rows_out].astype(o_ref.dtype)
        o_ref[i] = smooth
        masked = smooth * use_ref[...]
        m_ref[i] = masked
        wide = masked.astype(jnp.float32)
        partial = wide[0:8]
        for r in range(8, rows_out, 8):
            partial = partial + wide[r : r + 8]
        lanes = partial[:, 0:LANES]
        for c in range(LANES, cols_out, LANES):
            lanes = lanes + partial[:, c : c + LANES]
        s_ref[i] = lanes
        return carry

    lax.fori_loop(0, BAND_BLOCK, one_band, 0, unroll=UNROLL)


def smooth_both(center, tb, side, mask, use, kernel_one, kernel_two):
    bands, rows_out, cols_out = center.shape
    rows_in, cols_in = mask.shape
    smem = pltpu.SMEM
    return pl.pallas_call(
        smooth_kernel,
        grid=(bands // BAND_BLOCK,),
        in_specs=[
            pl.BlockSpec(memory_space=smem),
            pl.BlockSpec(memory_space=smem),
            pl.BlockSpec((rows_in, cols_in), lambda b: (0, 0)),
            pl.BlockSpec((rows_out, cols_out), lambda b: (0, 0)),
            pl.BlockSpec((BAND_BLOCK, rows_out, cols_out), lambda b: (b, 0, 0)),
            pl.BlockSpec((BAND_BLOCK, tb.shape[1], cols_out), lambda b: (b, 0, 0)),
            pl.BlockSpec((BAND_BLOCK, rows_in, side.shape[2]), lambda b: (b, 0, 0)),
        ],
        out_specs=[
            pl.BlockSpec((BAND_BLOCK, rows_out, cols_out), lambda b: (b, 0, 0)),
            pl.BlockSpec((BAND_BLOCK, rows_out, cols_out), lambda b: (b, 0, 0)),
            pl.BlockSpec((BAND_BLOCK, 8, LANES), lambda b: (b, 0, 0)),
        ],
        out_shape=[
            jax.ShapeDtypeStruct((bands, rows_out, cols_out), jnp.bfloat16),
            jax.ShapeDtypeStruct((bands, rows_out, cols_out), jnp.bfloat16),
            jax.ShapeDtypeStruct((bands, 8, LANES), jnp.float32),
        ],
        scratch_shapes=[pltpu.VMEM((rows_in, cols_in), jnp.float32)],
    )(kernel_one.reshape(-1), kernel_two.reshape(-1), mask, use, center, tb, side)


def tree_psum(value):
    for axis in ("along", "across"):
        size = lax.axis_size(axis)
        step = 1
        while step < size:
            pairs = [(i, i ^ step) for i in range(size)]
            value = value + lax.ppermute(value, axis, pairs)
            step *= 2
    return value


def lower_inverse(lower):
    size = lower.shape[0]
    half = size // 2
    eye = jnp.eye(half, dtype=lower.dtype)
    diagonal = jnp.stack([lower[:half, :half], lower[half:, half:]])
    inverses = lax.linalg.triangular_solve(
        diagonal, jnp.stack([eye, eye]), left_side=True, lower=True
    )
    top, bottom = inverses[0], inverses[1]
    high = lax.Precision.HIGHEST
    cross = -jnp.dot(bottom, jnp.dot(lower[half:, :half], top, precision=high), precision=high)
    return jnp.concatenate(
        [
            jnp.concatenate([top, jnp.zeros((half, size - half), lower.dtype)], axis=1),
            jnp.concatenate([cross, bottom], axis=1),
        ],
        axis=0,
    )


def per_device(radiance, kernel_one, kernel_two, usable_mask):
    band_count, tile_rows, tile_cols = radiance.shape
    n_across = lax.axis_size("across")
    n_along = lax.axis_size("along")
    col0 = lax.axis_index("across") * tile_cols
    row0 = lax.axis_index("along") * tile_rows

    top, bottom = shift_pair(radiance, "along", 1, HALO)
    tall = jnp.concatenate([radiance, bottom, top], axis=1)
    flat_strips = [
        lax.slice_in_dim(tall, start, start + HALO, axis=2).reshape(band_count, -1)
        for start in (tile_cols - HALO, 0)
    ]
    count_across = lax.axis_size("across")
    forward = [(i, i + 1) for i in range(count_across - 1)]
    backward = [(target, source) for source, target in forward]
    left = lax.ppermute(flat_strips[0], "across", forward).reshape(band_count, -1, HALO)
    right = lax.ppermute(flat_strips[1], "across", backward).reshape(band_count, -1, HALO)
    rows_in = tall.shape[1]
    gap = LANES - 2 * HALO
    side = jnp.concatenate(
        [right, jnp.zeros((band_count, rows_in, gap), right.dtype), left], axis=2
    )
    tb = jnp.concatenate([bottom, top], axis=1)
    cols_in = tile_cols + LANES

    pos_rows = lax.broadcasted_iota(jnp.int32, (rows_in, cols_in), 0)
    pos_cols = lax.broadcasted_iota(jnp.int32, (rows_in, cols_in), 1)
    mid_rows = jnp.where(pos_rows < tile_rows + HALO, pos_rows, pos_rows - rows_in) + row0
    mid_cols = jnp.where(pos_cols < tile_cols + LANES // 2, pos_cols, pos_cols - cols_in) + col0
    inside = (
        (mid_rows >= 0)
        & (mid_rows < n_along * tile_rows)
        & (mid_cols >= 0)
        & (mid_cols < n_across * tile_cols)
    )
    mid_mask = inside.astype(jnp.float32)

    use = usable_mask.astype(jnp.bfloat16)
    smoothed, masked, partial = smooth_both(
        radiance, tb, side, mid_mask, use, kernel_one, kernel_two
    )
    flat = masked.reshape(band_count, tile_rows * tile_cols)
    local_count = jnp.sum(usable_mask.astype(jnp.float32))
    local_sum = jnp.sum(partial, axis=(1, 2))
    local_gram = lax.dot_general(
        flat, flat, (((1,), (1,)), ((), ())), preferred_element_type=jnp.float32
    )
    half = band_count // 2
    upper_a = local_gram[:half, :half]
    lower_c = local_gram[half:, half:]
    rows = lax.broadcasted_iota(jnp.int32, (half, half), 0)
    cols = lax.broadcasted_iota(jnp.int32, (half, half), 1)
    below = rows >= cols
    on_diagonal = rows == cols
    folded = jnp.where(below, upper_a, lower_c)
    diagonal_c = jnp.sum(jnp.where(on_diagonal, lower_c, 0.0), axis=0)
    first_slot = lax.broadcasted_iota(jnp.int32, (band_count,), 0) == 0
    extra = jnp.concatenate(
        [
            local_sum[None],
            jnp.where(first_slot, local_count, 0.0)[None],
            jnp.concatenate([diagonal_c, jnp.zeros((band_count - half,), jnp.float32)])[None],
            jnp.zeros((5, band_count), jnp.float32),
        ],
        axis=0,
    )
    body = jnp.concatenate([local_gram[half:, :half], folded], axis=1)
    packed = tree_psum(jnp.concatenate([body, extra], axis=0))
    cross = packed[:half, :half]
    folded = packed[:half, half:]
    block_a = jnp.where(below, folded, 0.0) + jnp.where(rows > cols, folded, 0.0).T
    strict_up = jnp.where(below, 0.0, folded)
    block_c = (
        strict_up
        + strict_up.T
        + jnp.where(on_diagonal, packed[half + 2, :half][None, :], 0.0)
    )
    gram = jnp.concatenate(
        [
            jnp.concatenate([block_a, cross.T], axis=1),
            jnp.concatenate([cross, block_c], axis=1),
        ],
        axis=0,
    )
    band_sum = packed[half]
    count = packed[half + 1, 0]

    global_mean = band_sum / count
    covariance = (gram - count * jnp.outer(global_mean, global_mean)) / (count - 1.0)
    eye = jnp.eye(band_count, dtype=jnp.float32)
    loading = 0.01 * jnp.sum(jnp.where(eye > 0, covariance, 0.0)) / band_count
    loaded = covariance + loading * eye
    lower = jnp.linalg.cholesky(loaded, symmetrize_input=False)
    whitener = lower_inverse(lower)
    centered = (
        smoothed.astype(jnp.float32).reshape(band_count, tile_rows * tile_cols)
        - global_mean[:, None]
    )
    whitened = jnp.dot(
        whitener, centered, precision=lax.Precision.HIGH, preferred_element_type=jnp.float32
    )
    distance = jnp.sum(whitened * whitened, axis=0).reshape(tile_rows, tile_cols)
    standard = (distance - band_count) / math.sqrt(2.0 * band_count)
    return standard * usable_mask.astype(jnp.float32)


def solution(mesh):
    in_specs = (P(None, "along", "across"), P(), P(), P("along", "across"))
    out_specs = P("along", "across")
    return jax.shard_map(
        per_device, mesh=mesh, in_specs=in_specs, out_specs=out_specs, check_vma=False
    )
```

```python
import math

import jax
import jax.numpy as jnp
from jax import lax
from jax.experimental import pallas as pl
from jax.experimental.pallas import tpu as pltpu
from jax.sharding import PartitionSpec as P

KSIZE = 5
REACH = KSIZE // 2
HALO = 2 * REACH
LANES = 128
BAND_BLOCK = 16
UNROLL = 4


def shift_pair(block, axis, dim, width):
    count = lax.axis_size(axis)
    forward = [(i, i + 1) for i in range(count - 1)]
    backward = [(target, source) for source, target in forward]
    low = lax.ppermute(
        lax.slice_in_dim(block, block.shape[dim] - width, None, axis=dim), axis, forward
    )
    high = lax.ppermute(lax.slice_in_dim(block, 0, width, axis=dim), axis, backward)
    return low, high


def smooth_kernel(
    k1_ref, k2_ref, mask_ref, use_ref, x_ref, tb_ref, side_ref, o_ref, m_ref, s_ref, grid_ref
):
    block = pl.program_id(0)
    rows_in, cols_in = grid_ref.shape
    rows_out, cols_out = o_ref.shape[1], o_ref.shape[2]

    def correlate(x, taps, base, cols):
        total = None
        for p in range(KSIZE):
            part = None
            for q in range(KSIZE):
                shift = (REACH - q) % cols_in
                xq = pltpu.roll(x, shift, 1) if shift else x
                term = taps[base + p * KSIZE + q] * xq[:, :cols]
                part = term if part is None else part + term
            shift = (REACH - p) % rows_in
            if shift:
                part = pltpu.roll(part, shift, 0)
            total = part if total is None else total + part
        return total

    def one_band(i, carry):
        band = block * BAND_BLOCK + i
        base = band * (KSIZE * KSIZE)
        grid_ref[:rows_out, :cols_out] = x_ref[i].astype(jnp.float32)
        grid_ref[rows_out:, :cols_out] = tb_ref[i].astype(jnp.float32)
        grid_ref[:, cols_out:] = side_ref[i].astype(jnp.float32)
        x = grid_ref[...]
        first = correlate(x, k1_ref, base, cols_in) * mask_ref[...]
        second = correlate(first, k2_ref, base, cols_out)
        smooth = second[:rows_out].astype(o_ref.dtype)
        o_ref[i] = smooth
        masked = smooth * use_ref[...]
        m_ref[i] = masked
        wide = masked.astype(jnp.float32)
        partial = wide[0:8]
        for r in range(8, rows_out, 8):
            partial = partial + wide[r : r + 8]
        lanes = partial[:, 0:LANES]
        for c in range(LANES, cols_out, LANES):
            lanes = lanes + partial[:, c : c + LANES]
        s_ref[i] = lanes
        return carry

    lax.fori_loop(0, BAND_BLOCK, one_band, 0, unroll=UNROLL)


def smooth_both(center, tb, side, mask, use, kernel_one, kernel_two):
    bands, rows_out, cols_out = center.shape
    rows_in, cols_in = mask.shape
    smem = pltpu.SMEM
    return pl.pallas_call(
        smooth_kernel,
        grid=(bands // BAND_BLOCK,),
        in_specs=[
            pl.BlockSpec(memory_space=smem),
            pl.BlockSpec(memory_space=smem),
            pl.BlockSpec((rows_in, cols_in), lambda b: (0, 0)),
            pl.BlockSpec((rows_out, cols_out), lambda b: (0, 0)),
            pl.BlockSpec((BAND_BLOCK, rows_out, cols_out), lambda b: (b, 0, 0)),
            pl.BlockSpec((BAND_BLOCK, tb.shape[1], cols_out), lambda b: (b, 0, 0)),
            pl.BlockSpec((BAND_BLOCK, rows_in, side.shape[2]), lambda b: (b, 0, 0)),
        ],
        out_specs=[
            pl.BlockSpec((BAND_BLOCK, rows_out, cols_out), lambda b: (b, 0, 0)),
            pl.BlockSpec((BAND_BLOCK, rows_out, cols_out), lambda b: (b, 0, 0)),
            pl.BlockSpec((BAND_BLOCK, 8, LANES), lambda b: (b, 0, 0)),
        ],
        out_shape=[
            jax.ShapeDtypeStruct((bands, rows_out, cols_out), jnp.bfloat16),
            jax.ShapeDtypeStruct((bands, rows_out, cols_out), jnp.bfloat16),
            jax.ShapeDtypeStruct((bands, 8, LANES), jnp.float32),
        ],
        scratch_shapes=[pltpu.VMEM((rows_in, cols_in), jnp.float32)],
    )(kernel_one.reshape(-1), kernel_two.reshape(-1), mask, use, center, tb, side)


def tree_psum(value):
    for axis in ("along", "across"):
        size = lax.axis_size(axis)
        step = 1
        while step < size:
            pairs = [(i, i ^ step) for i in range(size)]
            value = value + lax.ppermute(value, axis, pairs)
            step *= 2
    return value


def lower_inverse(lower):
    size = lower.shape[0]
    half = size // 2
    eye = jnp.eye(half, dtype=lower.dtype)
    diagonal = jnp.stack([lower[:half, :half], lower[half:, half:]])
    inverses = lax.linalg.triangular_solve(
        diagonal, jnp.stack([eye, eye]), left_side=True, lower=True
    )
    top, bottom = inverses[0], inverses[1]
    high = lax.Precision.HIGHEST
    cross = -jnp.dot(bottom, jnp.dot(lower[half:, :half], top, precision=high), precision=high)
    return jnp.concatenate(
        [
            jnp.concatenate([top, jnp.zeros((half, size - half), lower.dtype)], axis=1),
            jnp.concatenate([cross, bottom], axis=1),
        ],
        axis=0,
    )


def per_device(radiance, kernel_one, kernel_two, usable_mask):
    band_count, tile_rows, tile_cols = radiance.shape
    n_across = lax.axis_size("across")
    n_along = lax.axis_size("along")
    col0 = lax.axis_index("across") * tile_cols
    row0 = lax.axis_index("along") * tile_rows

    top, bottom = shift_pair(radiance, "along", 1, HALO)
    tall = jnp.concatenate([radiance, bottom, top], axis=1)
    flat_strips = [
        lax.slice_in_dim(tall, start, start + HALO, axis=2).reshape(band_count, -1)
        for start in (tile_cols - HALO, 0)
    ]
    count_across = lax.axis_size("across")
    forward = [(i, i + 1) for i in range(count_across - 1)]
    backward = [(target, source) for source, target in forward]
    left = lax.ppermute(flat_strips[0], "across", forward).reshape(band_count, -1, HALO)
    right = lax.ppermute(flat_strips[1], "across", backward).reshape(band_count, -1, HALO)
    rows_in = tall.shape[1]
    gap = LANES - 2 * HALO
    side = jnp.concatenate(
        [right, jnp.zeros((band_count, rows_in, gap), right.dtype), left], axis=2
    )
    tb = jnp.concatenate([bottom, top], axis=1)
    cols_in = tile_cols + LANES

    pos_rows = lax.broadcasted_iota(jnp.int32, (rows_in, cols_in), 0)
    pos_cols = lax.broadcasted_iota(jnp.int32, (rows_in, cols_in), 1)
    mid_rows = jnp.where(pos_rows < tile_rows + HALO, pos_rows, pos_rows - rows_in) + row0
    mid_cols = jnp.where(pos_cols < tile_cols + LANES // 2, pos_cols, pos_cols - cols_in) + col0
    inside = (
        (mid_rows >= 0)
        & (mid_rows < n_along * tile_rows)
        & (mid_cols >= 0)
        & (mid_cols < n_across * tile_cols)
    )
    mid_mask = inside.astype(jnp.float32)

    use = usable_mask.astype(jnp.bfloat16)
    smoothed, masked, partial = smooth_both(
        radiance, tb, side, mid_mask, use, kernel_one, kernel_two
    )
    flat = masked.reshape(band_count, tile_rows * tile_cols)
    local_count = jnp.sum(usable_mask.astype(jnp.float32))
    local_sum = jnp.sum(partial, axis=(1, 2))
    local_gram = lax.dot_general(
        flat, flat, (((1,), (1,)), ((), ())), preferred_element_type=jnp.float32
    )
    half = band_count // 2
    upper_a = local_gram[:half, :half]
    lower_c = local_gram[half:, half:]
    rows = lax.broadcasted_iota(jnp.int32, (half, half), 0)
    cols = lax.broadcasted_iota(jnp.int32, (half, half), 1)
    below = rows >= cols
    on_diagonal = rows == cols
    folded = jnp.where(below, upper_a, lower_c)
    diagonal_c = jnp.sum(jnp.where(on_diagonal, lower_c, 0.0), axis=0)
    first_slot = lax.broadcasted_iota(jnp.int32, (band_count,), 0) == 0
    extra = jnp.concatenate(
        [
            local_sum[None],
            jnp.where(first_slot, local_count, 0.0)[None],
            jnp.concatenate([diagonal_c, jnp.zeros((band_count - half,), jnp.float32)])[None],
            jnp.zeros((5, band_count), jnp.float32),
        ],
        axis=0,
    )
    body = jnp.concatenate([local_gram[half:, :half], folded], axis=1)
    packed = tree_psum(jnp.concatenate([body, extra], axis=0))
    cross = packed[:half, :half]
    folded = packed[:half, half:]
    block_a = jnp.where(below, folded, 0.0) + jnp.where(rows > cols, folded, 0.0).T
    strict_up = jnp.where(below, 0.0, folded)
    block_c = (
        strict_up
        + strict_up.T
        + jnp.where(on_diagonal, packed[half + 2, :half][None, :], 0.0)
    )
    gram = jnp.concatenate(
        [
            jnp.concatenate([block_a, cross.T], axis=1),
            jnp.concatenate([cross, block_c], axis=1),
        ],
        axis=0,
    )
    band_sum = packed[half]
    count = packed[half + 1, 0]

    global_mean = band_sum / count
    covariance = (gram - count * jnp.outer(global_mean, global_mean)) / (count - 1.0)
    eye = jnp.eye(band_count, dtype=jnp.float32)
    loading = 0.01 * jnp.sum(jnp.where(eye > 0, covariance, 0.0)) / band_count
    loaded = covariance + loading * eye
    lower = jnp.linalg.cholesky(loaded, symmetrize_input=False)
    whitener = lower_inverse(lower)
    centered = smoothed.astype(jnp.float32) - global_mean[:, None, None]
    whitened = lax.dot_general(
        whitener,
        centered,
        (((1,), (0,)), ((), ())),
        precision=lax.Precision.HIGH,
        preferred_element_type=jnp.float32,
    )
    distance = jnp.sum(whitened * whitened, axis=0)
    standard = (distance - band_count) / math.sqrt(2.0 * band_count)
    return standard * usable_mask.astype(jnp.float32)


def solution(mesh):
    in_specs = (P(None, "along", "across"), P(), P(), P("along", "across"))
    out_specs = P("along", "across")
    return jax.shard_map(
        per_device, mesh=mesh, in_specs=in_specs, out_specs=out_specs, check_vma=False
    )
```
